256 devices in a mesh: dp: 32 (over x, z_hi, y), mp: 8 (over z_lo, core).
Axes of the slice: x: 4, y: 4, z: 8 (z_hi: 2, z_lo: 4; z = z_hi * 4 + z_lo), core: 2. Of those that a mesh axis runs over, the one named last changes fastest.
Arguments:
- forget_rows: bfloat16 [1024, 8192], P('dp', 'mp'), may hold values from -6 to 6
- cotangent: bfloat16 [1024, 8192], P('dp', 'mp'), may hold values from -6 to 6
- retain_rows: bfloat16 [1024, 8192], P('dp', 'mp'), may hold values from -6 to 6
- w_gate: bfloat16 [8192, 16384], P('mp', 'dp'), may hold values from -5 to 5
- w_up: bfloat16 [8192, 16384], P('mp', 'dp'), may hold values from -5 to 5
- w_down: bfloat16 [16384, 8192], P('dp', 'mp'), may hold values from -5 to 5
Outputs:
- retained: bfloat16 [1024, 8192], P('dp', 'mp')
- new_gate: bfloat16 [8192, 16384], P('mp', 'dp')
- new_up: bfloat16 [8192, 16384], P('mp', 'dp')
- new_down: bfloat16 [16384, 8192], P('dp', 'mp')
The draws below stay inside these ranges and needn't reach their ends.
All inputs are finite; a program needn't handle non-finite values.
Results may differ from the reference program's by a relative error of at most 0.0071.
Values may be sent and summed in bfloat16 or wider, within the bound.
No kernel may reach another device: no remote copies, remote signals or barrier semaphores. Data moves between devices by JAX's collectives and lax.ppermute only.
A program may use at most 64 MiB of HBM per device.

```python
import math
import jax
import jax.numpy as jnp

D = 8192
FF = 16384
TOKENS = 1024


def levels(rng, shape, split, low, largest):
    def one(dim, blocks):
        steps = jax.random.uniform(jax.random.fold_in(jax.random.fold_in(rng, 6), dim), (blocks,), jnp.float32, low / len(split), largest / len(split))
        return jnp.repeat(jnp.exp(steps), shape[dim] // blocks).reshape((-1,) + (1,) * (len(shape) - dim - 1))

    loudness = one(*split[0])
    for cut in split[1:]:
        loudness = loudness * one(*cut)
    return loudness


def scatter_about(stream_key, shape, scale, most, cuts=(), kind=jnp.bfloat16):
    entries = scale * jax.random.normal(stream_key, shape, jnp.float32)
    if cuts:
        entries = entries * levels(stream_key, shape, cuts, -0.22, 0.18)
    return jnp.clip(entries, -most, most).astype(kind)


def setup_inputs(seed: int = 0) -> dict:
    splits = jax.random.split(jax.random.key(seed), 7)
    forget_rows = scatter_about(splits[0], (TOKENS, D), 1.0, 6.0, ((0, 32), (1, 8)))
    cotangent = scatter_about(splits[1], (TOKENS, D), 1.0, 6.0, ((0, 32), (1, 8)))
    retain_rows = scatter_about(splits[2], (TOKENS, D), 1.0, 6.0, ((0, 32), (1, 8)))
    w_gate = scatter_about(splits[3], (D, FF), 1.0, 5.0, ((0, 8), (1, 32)))
    w_up = scatter_about(splits[4], (D, FF), 1.0, 5.0, ((0, 8), (1, 32)))
    w_down = scatter_about(splits[5], (FF, D), 1.0, 5.0, ((0, 32), (1, 8)))
    return dict(forget_rows=forget_rows, cotangent=cotangent, retain_rows=retain_rows, w_gate=w_gate, w_up=w_up, w_down=w_down)


STEP_SIZE = 0.5

def unit_forward(rows, gate_weight, up_weight):
    width_scale = 1.0 / math.sqrt(D)
    gate_sum = jnp.dot(rows, gate_weight, preferred_element_type=jnp.float32) * width_scale
    up_sum = jnp.dot(rows, up_weight, preferred_element_type=jnp.float32) * width_scale
    sigmoid_gate = jax.nn.sigmoid(gate_sum)
    return (gate_sum, up_sum, sigmoid_gate, gate_sum * sigmoid_gate)

def reference(forget_rows, cotangent, retain_rows, w_gate, w_up, w_down):
    token_scale = 1.0 / math.sqrt(TOKENS)
    gate_sum, up_sum, sigmoid_gate, active = unit_forward(forget_rows, w_gate, w_up)
    hidden = (active * up_sum).astype(jnp.bfloat16)
    grad_down = jnp.dot(hidden.T, cotangent, preferred_element_type=jnp.float32) * token_scale
    new_down = (w_down.astype(jnp.float32) + STEP_SIZE * grad_down).astype(jnp.bfloat16)
    back_units = jnp.dot(cotangent, w_down.T, preferred_element_type=jnp.float32) * (1.0 / math.sqrt(D))
    grad_gate_units = (back_units * up_sum * sigmoid_gate * (1.0 + gate_sum * (1.0 - sigmoid_gate))).astype(jnp.bfloat16)
    grad_up_units = (back_units * active).astype(jnp.bfloat16)
    grad_gate = jnp.dot(forget_rows.T, grad_gate_units, preferred_element_type=jnp.float32) * token_scale
    new_gate = (w_gate.astype(jnp.float32) + STEP_SIZE * grad_gate).astype(jnp.bfloat16)
    grad_up = jnp.dot(forget_rows.T, grad_up_units, preferred_element_type=jnp.float32) * token_scale
    new_up = (w_up.astype(jnp.float32) + STEP_SIZE * grad_up).astype(jnp.bfloat16)
    gate_keep, up_keep, sigmoid_keep, active_keep = unit_forward(retain_rows, new_gate, new_up)
    hidden_keep = (active_keep * up_keep).astype(jnp.bfloat16)
    retained = jnp.dot(hidden_keep, new_down, preferred_element_type=jnp.float32) * (1.0 / math.sqrt(FF))
    return (retained.astype(jnp.bfloat16), new_gate, new_up, new_down)
```

```python
import math

import jax
import jax.numpy as jnp
from jax import lax
from jax.sharding import Mesh
from jax.sharding import PartitionSpec as P

D = 8192
FF = 16384


STEP_SIZE = 0.5

DP = ("x", "zh", "y")
MP = ("zl", "c")


def shift(v, axis, n, k):
    return lax.ppermute(v, axis, [(i, (i + k) % n) for i in range(n)])


def gather_ring(blocks, axis, n):
    if n == 2:
        return jnp.stack([blocks, shift(blocks, axis, 2, 1)])
    half = blocks.shape[-1] // 2
    left = shift(blocks, axis, n, 1)
    right = shift(blocks, axis, n, -1)
    far = jnp.concatenate(
        [shift(left[..., :half], axis, n, 1), shift(right[..., half:], axis, n, -1)], axis=-1
    )
    return jnp.stack([blocks, left, far, right])


def scatter_ring(parts, axis, n):
    send = lambda v, k: shift(v.astype(jnp.bfloat16), axis, n, k).astype(jnp.float32)
    if n == 2:
        return parts[0] + send(parts[1], 1)
    half = parts.shape[-1] // 2
    near = parts[1].at[..., :half].add(send(parts[2][..., :half], -1))
    back = parts[3].at[..., half:].add(send(parts[2][..., half:], 1))
    return parts[0] + send(near, -1) + send(back, 1)


def gather_tokens(rows):
    half = rows.shape[1] // 2
    first = gather_ring(gather_ring(gather_ring(rows[:, :half], "zh", 2), "y", 4), "x", 4)
    second = gather_ring(gather_ring(gather_ring(rows[:, half:], "zh", 2), "x", 4), "y", 4)
    second = jnp.swapaxes(second, 0, 1)
    whole = jnp.concatenate([first, second], axis=-1)
    return whole.reshape(-1, rows.shape[1])


def scatter_tokens(sums, t):
    half = sums.shape[1] // 2
    parts = sums.reshape(4, 4, 2, t, sums.shape[1])
    first = scatter_ring(scatter_ring(scatter_ring(parts[..., :half], "x", 4), "y", 4), "zh", 2)
    second = jnp.swapaxes(parts[..., half:], 0, 1)
    second = scatter_ring(scatter_ring(scatter_ring(second, "y", 4), "x", 4), "zh", 2)
    return jnp.concatenate([first, second], axis=-1)


def project_sum(rows_all, weight_pair):
    width_scale = 1.0 / math.sqrt(D)
    return lax.psum_scatter(
        jnp.dot(rows_all, weight_pair, preferred_element_type=jnp.float32) * width_scale,
        MP,
        scatter_dimension=0,
        tiled=True,
    )


def gather_units(values):
    return lax.all_gather(values, MP, axis=0, tiled=True)


def activate(sums, unit_count):
    gate_sum = sums[:, :unit_count]
    up_sum = sums[:, unit_count:]
    sigmoid_gate = jax.nn.sigmoid(gate_sum)
    return (gate_sum, up_sum, sigmoid_gate, gate_sum * sigmoid_gate)


def unit_grads(back_units, gate_sum, up_sum, sigmoid_gate, active):
    grad_gate = back_units * up_sum * sigmoid_gate * (1.0 + gate_sum * (1.0 - sigmoid_gate))
    grad_up = back_units * active
    return jnp.concatenate([grad_gate, grad_up], axis=1).astype(jnp.bfloat16)


def body(forget_rows, cotangent, retain_rows, w_gate, w_up, w_down):
    unit_count = w_gate.shape[1]
    local_rows, width = forget_rows.shape
    width_scale = 1.0 / math.sqrt(D)
    contract_rows = (((0,), (0,)), ((), ()))
    contract_cols = (((1,), (1,)), ((), ()))
    gathered = gather_tokens(jnp.concatenate([forget_rows, cotangent, retain_rows], axis=1))
    forget_all = gathered[:, :width]
    cotan_all = gathered[:, width : 2 * width]
    retain_all = gathered[:, 2 * width :]
    total_rows = forget_all.shape[0]
    token_scale = 1.0 / math.sqrt(total_rows)
    weight_pair = jnp.concatenate([w_gate, w_up], axis=1)
    sums = project_sum(forget_all, weight_pair)
    gate_sum, up_sum, sigmoid_gate, active = activate(sums, unit_count)
    hidden = (active * up_sum).astype(jnp.bfloat16)
    hidden_all = gather_units(hidden)
    back_units = lax.psum_scatter(
        lax.dot_general(cotan_all, w_down, contract_cols, preferred_element_type=jnp.float32)
        * width_scale,
        MP,
        scatter_dimension=0,
        tiled=True,
    )
    grads_all = gather_units(unit_grads(back_units, gate_sum, up_sum, sigmoid_gate, active))
    grad_down = (
        lax.dot_general(hidden_all, cotan_all, contract_rows, preferred_element_type=jnp.float32)
        * token_scale
    )
    grad_pair = (
        lax.dot_general(forget_all, grads_all, contract_rows, preferred_element_type=jnp.float32)
        * token_scale
    )
    new_gate = (w_gate.astype(jnp.float32) + STEP_SIZE * grad_pair[:, :unit_count]).astype(
        jnp.bfloat16
    )
    new_up = (w_up.astype(jnp.float32) + STEP_SIZE * grad_pair[:, unit_count:]).astype(jnp.bfloat16)
    new_down = (w_down.astype(jnp.float32) + STEP_SIZE * grad_down).astype(jnp.bfloat16)
    new_pair = jnp.concatenate([new_gate, new_up], axis=1)
    keep_sums = project_sum(retain_all, new_pair)
    gate_keep, up_keep, sigmoid_keep, active_keep = activate(keep_sums, unit_count)
    hidden_keep = (active_keep * up_keep).astype(jnp.bfloat16)
    hidden_keep_all = gather_units(hidden_keep)
    out_scale = 1.0 / math.sqrt(FF)
    partial = jnp.dot(hidden_keep_all, new_down, preferred_element_type=jnp.float32) * out_scale
    retained = scatter_tokens(partial, local_rows).astype(jnp.bfloat16)
    return (retained, new_gate, new_up, new_down)


def solution(mesh):
    dp_size, mp_size = mesh.devices.shape
    physical = Mesh(mesh.devices.reshape(dp_size // 8, 2, 4, mp_size // 2, 2), DP + MP)
    rows = P(DP, MP)
    cols = P(MP, DP)
    in_specs = (rows, rows, rows, cols, cols, rows)
    out_specs = (rows, cols, cols, rows)
    return jax.shard_map(body, mesh=physical, in_specs=in_specs, out_specs=out_specs, check_vma=False)
```

```python
import math

import jax
import jax.numpy as jnp
from jax import lax
from jax.sharding import Mesh
from jax.sharding import PartitionSpec as P

D = 8192
FF = 16384


STEP_SIZE = 0.5

DP = ("x", "zh", "y")
MP = ("zl", "c")


def shift(v, axis, n, k):
    return lax.ppermute(v, axis, [(i, (i + k) % n) for i in range(n)])


def gather_ring(blocks, axis, n):
    if n == 2:
        return jnp.stack([blocks, shift(blocks, axis, 2, 1)])
    half = blocks.shape[-1] // 2
    left = shift(blocks, axis, n, 1)
    right = shift(blocks, axis, n, -1)
    far = jnp.concatenate(
        [shift(left[..., :half], axis, n, 1), shift(right[..., half:], axis, n, -1)], axis=-1
    )
    return jnp.stack([blocks, left, far, right])


def scatter_ring(parts, axis, n):
    send = lambda v, k: shift(v.astype(jnp.bfloat16), axis, n, k).astype(jnp.float32)
    if n == 2:
        return parts[0] + send(parts[1], 1)
    half = parts.shape[-1] // 2
    near = parts[1].at[..., :half].add(send(parts[2][..., :half], -1))
    back = parts[3].at[..., half:].add(send(parts[2][..., half:], 1))
    return parts[0] + send(near, -1) + send(back, 1)


def gather_tokens(rows):
    half = rows.shape[1] // 2
    first = gather_ring(gather_ring(gather_ring(rows[:, :half], "zh", 2), "y", 4), "x", 4)
    second = gather_ring(gather_ring(gather_ring(rows[:, half:], "zh", 2), "x", 4), "y", 4)
    second = jnp.swapaxes(second, 0, 1)
    whole = jnp.concatenate([first, second], axis=-1)
    return whole.reshape(-1, rows.shape[1])


def scatter_tokens(sums, t):
    half = sums.shape[1] // 2
    parts = sums.reshape(4, 4, 2, t, sums.shape[1])
    first = scatter_ring(scatter_ring(scatter_ring(parts[..., :half], "x", 4), "y", 4), "zh", 2)
    second = jnp.swapaxes(parts[..., half:], 0, 1)
    second = scatter_ring(scatter_ring(scatter_ring(second, "y", 4), "x", 4), "zh", 2)
    return jnp.concatenate([first, second], axis=-1)


def gather_units(values):
    zl = lax.axis_index("zl")
    right, left, got_right, got_left = values, values, [], []
    for step in range(1, 4):
        right = lax.ppermute(right, "zl", [(k, k + 1) for k in range(step - 1, 3)])
        left = lax.ppermute(left, "zl", [(k, k - 1) for k in range(1, 5 - step)])
        got_right.append(right)
        got_left.append(left)
    line = jnp.stack(got_right[::-1] + [values] + got_left)
    blocks = lax.dynamic_slice_in_dim(line, 3 - zl, 4, axis=0)
    other = lax.ppermute(blocks, "c", [(0, 1), (1, 0)])
    first = lax.axis_index("c") == 0
    whole = jnp.where(first, jnp.stack([blocks, other], 1), jnp.stack([other, blocks], 1))
    return whole.reshape(-1, values.shape[1])


def scatter_units(sums):
    t = sums.shape[0] // 8
    parts = sums.reshape(4, 2, t, sums.shape[1])
    core = lax.axis_index("c")
    mine = lax.dynamic_index_in_dim(parts, core, axis=1, keepdims=False)
    other = lax.dynamic_index_in_dim(parts, 1 - core, axis=1, keepdims=False)
    chip = mine + lax.ppermute(other, "c", [(0, 1), (1, 0)])
    zl = lax.axis_index("zl")
    pick = lambda b: lax.dynamic_index_in_dim(chip, jnp.clip(b, 0, 3), axis=0, keepdims=False)
    from_left = jnp.zeros_like(chip[0])
    from_right = jnp.zeros_like(chip[0])
    for step in range(1, 4):
        to_right = pick(4 + zl - step) + from_left
        to_left = pick(zl + step - 4) + from_right
        from_left = lax.ppermute(to_right, "zl", [(k, k + 1) for k in range(step)])
        from_right = lax.ppermute(to_left, "zl", [(k, k - 1) for k in range(4 - step, 4)])
    return pick(zl) + from_left + from_right


def project_sum(rows_all, weight_pair):
    width_scale = 1.0 / math.sqrt(D)
    return scatter_units(
        jnp.dot(rows_all, weight_pair, preferred_element_type=jnp.float32) * width_scale
    )


def activate(sums, unit_count):
    gate_sum = sums[:, :unit_count]
    up_sum = sums[:, unit_count:]
    sigmoid_gate = jax.nn.sigmoid(gate_sum)
    return (gate_sum, up_sum, sigmoid_gate, gate_sum * sigmoid_gate)


def unit_grads(back_units, gate_sum, up_sum, sigmoid_gate, active):
    grad_gate = back_units * up_sum * sigmoid_gate * (1.0 + gate_sum * (1.0 - sigmoid_gate))
    grad_up = back_units * active
    return jnp.concatenate([grad_gate, grad_up], axis=1).astype(jnp.bfloat16)


def body(forget_rows, cotangent, retain_rows, w_gate, w_up, w_down):
    unit_count = w_gate.shape[1]
    local_rows, width = forget_rows.shape
    width_scale = 1.0 / math.sqrt(D)
    contract_rows = (((0,), (0,)), ((), ()))
    contract_cols = (((1,), (1,)), ((), ()))
    gathered = gather_tokens(jnp.concatenate([forget_rows, cotangent, retain_rows], axis=1))
    forget_all = gathered[:, :width]
    cotan_all = gathered[:, width : 2 * width]
    retain_all = gathered[:, 2 * width :]
    total_rows = forget_all.shape[0]
    token_scale = 1.0 / math.sqrt(total_rows)
    weight_pair = jnp.concatenate([w_gate, w_up], axis=1)
    sums = project_sum(forget_all, weight_pair)
    gate_sum, up_sum, sigmoid_gate, active = activate(sums, unit_count)
    hidden = (active * up_sum).astype(jnp.bfloat16)
    hidden_all = gather_units(hidden)
    back_units = scatter_units(
        lax.dot_general(cotan_all, w_down, contract_cols, preferred_element_type=jnp.float32)
        * width_scale
    )
    grads_all = gather_units(unit_grads(back_units, gate_sum, up_sum, sigmoid_gate, active))
    grad_down = (
        lax.dot_general(hidden_all, cotan_all, contract_rows, preferred_element_type=jnp.float32)
        * token_scale
    )
    grad_pair = (
        lax.dot_general(forget_all, grads_all, contract_rows, preferred_element_type=jnp.float32)
        * token_scale
    )
    new_gate = (w_gate.astype(jnp.float32) + STEP_SIZE * grad_pair[:, :unit_count]).astype(
        jnp.bfloat16
    )
    new_up = (w_up.astype(jnp.float32) + STEP_SIZE * grad_pair[:, unit_count:]).astype(jnp.bfloat16)
    new_down = (w_down.astype(jnp.float32) + STEP_SIZE * grad_down).astype(jnp.bfloat16)
    new_pair = jnp.concatenate([new_gate, new_up], axis=1)
    keep_sums = project_sum(retain_all, new_pair)
    gate_keep, up_keep, sigmoid_keep, active_keep = activate(keep_sums, unit_count)
    hidden_keep = (active_keep * up_keep).astype(jnp.bfloat16)
    hidden_keep_all = gather_units(hidden_keep)
    out_scale = 1.0 / math.sqrt(FF)
    partial = jnp.dot(hidden_keep_all, new_down, preferred_element_type=jnp.float32) * out_scale
    retained = scatter_tokens(partial, local_rows).astype(jnp.bfloat16)
    return (retained, new_gate, new_up, new_down)


def solution(mesh):
    dp_size, mp_size = mesh.devices.shape
    physical = Mesh(mesh.devices.reshape(dp_size // 8, 2, 4, mp_size // 2, 2), DP + MP)
    rows = P(DP, MP)
    cols = P(MP, DP)
    in_specs = (rows, rows, rows, cols, cols, rows)
    out_specs = (rows, cols, cols, rows)
    return jax.shard_map(body, mesh=physical, in_specs=in_specs, out_specs=out_specs, check_vma=False)
```

```python
import math

import jax
import jax.numpy as jnp
from jax import lax
from jax.sharding import Mesh
from jax.sharding import PartitionSpec as P

D = 8192
FF = 16384


STEP_SIZE = 0.5

DP = ("x", "zh", "y")
MP = ("zl", "c")


def shift(v, axis, n, k):
    return lax.ppermute(v, axis, [(i, (i + k) % n) for i in range(n)])


def gather_ring(blocks, axis, n):
    if n == 2:
        return jnp.stack([blocks, shift(blocks, axis, 2, 1)])
    half = blocks.shape[-1] // 2
    left = shift(blocks, axis, n, 1)
    right = shift(blocks, axis, n, -1)
    far = jnp.concatenate(
        [shift(left[..., :half], axis, n, 1), shift(right[..., half:], axis, n, -1)], axis=-1
    )
    return jnp.stack([blocks, left, far, right])


def scatter_ring(parts, axis, n):
    send = lambda v, k: shift(v, axis, n, k)
    if n == 2:
        return parts[0] + send(parts[1], 1)
    half = parts.shape[-1] // 2
    near = parts[1].at[..., :half].add(send(parts[2][..., :half], -1))
    back = parts[3].at[..., half:].add(send(parts[2][..., half:], 1))
    return parts[0] + send(near, -1) + send(back, 1)


def gather_tokens(rows):
    half = rows.shape[1] // 2
    first = gather_ring(gather_ring(gather_ring(rows[:, :half], "zh", 2), "y", 4), "x", 4)
    second = gather_ring(gather_ring(gather_ring(rows[:, half:], "zh", 2), "x", 4), "y", 4)
    second = jnp.swapaxes(second, 0, 1)
    whole = jnp.concatenate([first, second], axis=-1)
    return whole.reshape(-1, rows.shape[1])


def scatter_tokens(sums, t):
    half = sums.shape[1] // 2
    parts = sums.reshape(4, 4, 2, t, sums.shape[1])
    first = scatter_ring(scatter_ring(scatter_ring(parts[..., :half], "x", 4), "y", 4), "zh", 2)
    second = jnp.swapaxes(parts[..., half:], 0, 1)
    second = scatter_ring(scatter_ring(scatter_ring(second, "y", 4), "x", 4), "zh", 2)
    return jnp.concatenate([first, second], axis=-1)


def gather_units(values):
    zl = lax.axis_index("zl")
    right, left, got_right, got_left = values, values, [], []
    for step in range(1, 4):
        right = lax.ppermute(right, "zl", [(k, k + 1) for k in range(step - 1, 3)])
        left = lax.ppermute(left, "zl", [(k, k - 1) for k in range(1, 5 - step)])
        got_right.append(right)
        got_left.append(left)
    line = jnp.stack(got_right[::-1] + [values] + got_left)
    blocks = lax.dynamic_slice_in_dim(line, 3 - zl, 4, axis=0)
    other = lax.ppermute(blocks, "c", [(0, 1), (1, 0)])
    first = lax.axis_index("c") == 0
    whole = jnp.where(first, jnp.stack([blocks, other], 1), jnp.stack([other, blocks], 1))
    return whole.reshape(-1, values.shape[1])


def scatter_units(sums):
    t = sums.shape[0] // 8
    parts = sums.reshape(4, 2, t, sums.shape[1])
    core = lax.axis_index("c")
    mine = lax.dynamic_index_in_dim(parts, core, axis=1, keepdims=False)
    other = lax.dynamic_index_in_dim(parts, 1 - core, axis=1, keepdims=False)
    send = lambda v, axis, pairs: lax.ppermute(v.astype(jnp.bfloat16), axis, pairs).astype(jnp.float32)
    chip = mine + send(other, "c", [(0, 1), (1, 0)])
    zl = lax.axis_index("zl")
    pick = lambda b: lax.dynamic_index_in_dim(chip, jnp.clip(b, 0, 3), axis=0, keepdims=False)
    from_left = jnp.zeros_like(chip[0])
    from_right = jnp.zeros_like(chip[0])
    for step in range(1, 4):
        to_right = pick(4 + zl - step) + from_left
        to_left = pick(zl + step - 4) + from_right
        from_left = send(to_right, "zl", [(k, k + 1) for k in range(step)])
        from_right = send(to_left, "zl", [(k, k - 1) for k in range(4 - step, 4)])
    return pick(zl) + from_left + from_right


def project_sum(rows_all, weight_pair):
    width_scale = 1.0 / math.sqrt(D)
    return scatter_units(
        jnp.dot(rows_all, weight_pair, preferred_element_type=jnp.float32) * width_scale
    )


def activate(sums, unit_count):
    gate_sum = sums[:, :unit_count]
    up_sum = sums[:, unit_count:]
    sigmoid_gate = jax.nn.sigmoid(gate_sum)
    return (gate_sum, up_sum, sigmoid_gate, gate_sum * sigmoid_gate)


def unit_grads(back_units, gate_sum, up_sum, sigmoid_gate, active):
    grad_gate = back_units * up_sum * sigmoid_gate * (1.0 + gate_sum * (1.0 - sigmoid_gate))
    grad_up = back_units * active
    return jnp.concatenate([grad_gate, grad_up], axis=1).astype(jnp.bfloat16)


def body(forget_rows, cotangent, retain_rows, w_gate, w_up, w_down):
    unit_count = w_gate.shape[1]
    local_rows, width = forget_rows.shape
    width_scale = 1.0 / math.sqrt(D)
    contract_rows = (((0,), (0,)), ((), ()))
    contract_cols = (((1,), (1,)), ((), ()))
    gathered = gather_tokens(jnp.concatenate([forget_rows, cotangent], axis=1))
    forget_all = gathered[:, :width]
    cotan_all = gathered[:, width:]
    retain_all = gather_tokens(retain_rows)
    total_rows = forget_all.shape[0]
    token_scale = 1.0 / math.sqrt(total_rows)
    weight_pair = jnp.concatenate([w_gate, w_up], axis=1)
    sums = project_sum(forget_all, weight_pair)
    gate_sum, up_sum, sigmoid_gate, active = activate(sums, unit_count)
    hidden = (active * up_sum).astype(jnp.bfloat16)
    hidden_all = gather_units(hidden)
    back_units = scatter_units(
        lax.dot_general(cotan_all, w_down, contract_cols, preferred_element_type=jnp.float32)
        * width_scale
    )
    grads_all = gather_units(unit_grads(back_units, gate_sum, up_sum, sigmoid_gate, active))
    grad_down = (
        lax.dot_general(hidden_all, cotan_all, contract_rows, preferred_element_type=jnp.float32)
        * token_scale
    )
    grad_pair = (
        lax.dot_general(forget_all, grads_all, contract_rows, preferred_element_type=jnp.float32)
        * token_scale
    )
    new_gate = (w_gate.astype(jnp.float32) + STEP_SIZE * grad_pair[:, :unit_count]).astype(
        jnp.bfloat16
    )
    new_up = (w_up.astype(jnp.float32) + STEP_SIZE * grad_pair[:, unit_count:]).astype(jnp.bfloat16)
    new_down = (w_down.astype(jnp.float32) + STEP_SIZE * grad_down).astype(jnp.bfloat16)
    new_pair = jnp.concatenate([new_gate, new_up], axis=1)
    keep_sums = project_sum(retain_all, new_pair)
    gate_keep, up_keep, sigmoid_keep, active_keep = activate(keep_sums, unit_count)
    hidden_keep = (active_keep * up_keep).astype(jnp.bfloat16)
    hidden_keep_all = gather_units(hidden_keep)
    out_scale = 1.0 / math.sqrt(FF)
    partial = jnp.dot(hidden_keep_all, new_down, preferred_element_type=jnp.float32) * out_scale
    retained = scatter_tokens(partial, local_rows).astype(jnp.bfloat16)
    return (retained, new_gate, new_up, new_down)


def solution(mesh):
    dp_size, mp_size = mesh.devices.shape
    physical = Mesh(mesh.devices.reshape(dp_size // 8, 2, 4, mp_size // 2, 2), DP + MP)
    rows = P(DP, MP)
    cols = P(MP, DP)
    in_specs = (rows, rows, rows, cols, cols, rows)
    out_specs = (rows, cols, cols, rows)
    return jax.shard_map(body, mesh=physical, in_specs=in_specs, out_specs=out_specs, check_vma=False)
```

```python
import math

import jax
import jax.numpy as jnp
from jax import lax
from jax.sharding import Mesh
from jax.sharding import PartitionSpec as P

D = 8192
FF = 16384


STEP_SIZE = 0.5

DP = ("x", "zh", "y")
MP = ("zl", "c")


def shift(v, axis, n, k):
    return lax.ppermute(v, axis, [(i, (i + k) % n) for i in range(n)])


def gather_ring(blocks, axis, n):
    if n == 2:
        return jnp.stack([blocks, shift(blocks, axis, 2, 1)])
    half = blocks.shape[-1] // 2
    left = shift(blocks, axis, n, 1)
    right = shift(blocks, axis, n, -1)
    far = jnp.concatenate(
        [shift(left[..., :half], axis, n, 1), shift(right[..., half:], axis, n, -1)], axis=-1
    )
    return jnp.stack([blocks, left, far, right])


def scatter_ring(parts, axis, n):
    send = lambda v, k: shift(v, axis, n, k)
    if n == 2:
        return parts[0] + send(parts[1], 1)
    half = parts.shape[-1] // 2
    near = parts[1].at[..., :half].add(send(parts[2][..., :half], -1))
    back = parts[3].at[..., half:].add(send(parts[2][..., half:], 1))
    return parts[0] + send(near, -1) + send(back, 1)


def gather_tokens(rows):
    half = rows.shape[1] // 2
    first = gather_ring(gather_ring(gather_ring(rows[:, :half], "zh", 2), "y", 4), "x", 4)
    second = gather_ring(gather_ring(gather_ring(rows[:, half:], "zh", 2), "x", 4), "y", 4)
    second = jnp.swapaxes(second, 0, 1)
    whole = jnp.concatenate([first, second], axis=-1)
    return whole.reshape(-1, rows.shape[1])


def scatter_tokens(sums, t):
    half = sums.shape[1] // 2
    parts = sums.reshape(4, 4, 2, t, sums.shape[1])
    first = scatter_ring(scatter_ring(scatter_ring(parts[..., :half], "x", 4), "y", 4), "zh", 2)
    second = jnp.swapaxes(parts[..., half:], 0, 1)
    second = scatter_ring(scatter_ring(scatter_ring(second, "y", 4), "x", 4), "zh", 2)
    return jnp.concatenate([first, second], axis=-1)


def gather_units(values):
    zl = lax.axis_index("zl")
    right, left, got_right, got_left = values, values, [], []
    for step in range(1, 4):
        right = lax.ppermute(right, "zl", [(k, k + 1) for k in range(step - 1, 3)])
        left = lax.ppermute(left, "zl", [(k, k - 1) for k in range(1, 5 - step)])
        got_right.append(right)
        got_left.append(left)
    line = jnp.stack(got_right[::-1] + [values] + got_left)
    blocks = lax.dynamic_slice_in_dim(line, 3 - zl, 4, axis=0)
    other = lax.ppermute(blocks, "c", [(0, 1), (1, 0)])
    first = lax.axis_index("c") == 0
    whole = jnp.where(first, jnp.stack([blocks, other], 1), jnp.stack([other, blocks], 1))
    return whole.reshape(-1, values.shape[1])


def scatter_units(sums):
    t = sums.shape[0] // 8
    parts = sums.reshape(4, 2, t, sums.shape[1])
    core = lax.axis_index("c")
    mine = lax.dynamic_index_in_dim(parts, core, axis=1, keepdims=False)
    other = lax.dynamic_index_in_dim(parts, 1 - core, axis=1, keepdims=False)
    send = lax.ppermute
    chip = mine + send(other, "c", [(0, 1), (1, 0)])
    zl = lax.axis_index("zl")
    pick = lambda b: lax.dynamic_index_in_dim(chip, jnp.clip(b, 0, 3), axis=0, keepdims=False)
    from_left = jnp.zeros_like(chip[0])
    from_right = jnp.zeros_like(chip[0])
    for step in range(1, 4):
        to_right = pick(4 + zl - step) + from_left
        to_left = pick(zl + step - 4) + from_right
        from_left = send(to_right, "zl", [(k, k + 1) for k in range(step)])
        from_right = send(to_left, "zl", [(k, k - 1) for k in range(4 - step, 4)])
    return pick(zl) + from_left + from_right


def project_sum(rows_all, weight_pair):
    width_scale = 1.0 / math.sqrt(D)
    return scatter_units(
        jnp.dot(rows_all, weight_pair, preferred_element_type=jnp.float32) * width_scale
    )


def activate(sums, unit_count):
    gate_sum = sums[:, :unit_count]
    up_sum = sums[:, unit_count:]
    sigmoid_gate = jax.nn.sigmoid(gate_sum)
    return (gate_sum, up_sum, sigmoid_gate, gate_sum * sigmoid_gate)


def unit_grads(back_units, gate_sum, up_sum, sigmoid_gate, active):
    grad_gate = back_units * up_sum * sigmoid_gate * (1.0 + gate_sum * (1.0 - sigmoid_gate))
    grad_up = back_units * active
    return jnp.concatenate([grad_gate, grad_up], axis=1).astype(jnp.bfloat16)


def body(forget_rows, cotangent, retain_rows, w_gate, w_up, w_down):
    unit_count = w_gate.shape[1]
    local_rows, width = forget_rows.shape
    width_scale = 1.0 / math.sqrt(D)
    contract_rows = (((0,), (0,)), ((), ()))
    contract_cols = (((1,), (1,)), ((), ()))
    gathered = gather_tokens(jnp.concatenate([forget_rows, cotangent], axis=1))
    forget_all = gathered[:, :width]
    cotan_all = gathered[:, width:]
    retain_all = gather_tokens(retain_rows)
    total_rows = forget_all.shape[0]
    token_scale = 1.0 / math.sqrt(total_rows)
    weight_pair = jnp.concatenate([w_gate, w_up], axis=1)
    forward = jnp.dot(forget_all, weight_pair, preferred_element_type=jnp.float32)
    backward = lax.dot_general(cotan_all, w_down, contract_cols, preferred_element_type=jnp.float32)
    both = scatter_units(jnp.concatenate([forward, backward], axis=1) * width_scale)
    gate_sum, up_sum, sigmoid_gate, active = activate(both[:, : 2 * unit_count], unit_count)
    back_units = both[:, 2 * unit_count :]
    hidden = (active * up_sum).astype(jnp.bfloat16)
    units_all = gather_units(
        jnp.concatenate([hidden, unit_grads(back_units, gate_sum, up_sum, sigmoid_gate, active)], axis=1)
    )
    hidden_all = units_all[:, :unit_count]
    grads_all = units_all[:, unit_count:]
    grad_down = (
        lax.dot_general(hidden_all, cotan_all, contract_rows, preferred_element_type=jnp.float32)
        * token_scale
    )
    grad_pair = (
        lax.dot_general(forget_all, grads_all, contract_rows, preferred_element_type=jnp.float32)
        * token_scale
    )
    new_gate = (w_gate.astype(jnp.float32) + STEP_SIZE * grad_pair[:, :unit_count]).astype(
        jnp.bfloat16
    )
    new_up = (w_up.astype(jnp.float32) + STEP_SIZE * grad_pair[:, unit_count:]).astype(jnp.bfloat16)
    new_down = (w_down.astype(jnp.float32) + STEP_SIZE * grad_down).astype(jnp.bfloat16)
    new_pair = jnp.concatenate([new_gate, new_up], axis=1)
    keep_sums = project_sum(retain_all, new_pair)
    gate_keep, up_keep, sigmoid_keep, active_keep = activate(keep_sums, unit_count)
    hidden_keep = (active_keep * up_keep).astype(jnp.bfloat16)
    hidden_keep_all = gather_units(hidden_keep)
    out_scale = 1.0 / math.sqrt(FF)
    partial = jnp.dot(hidden_keep_all, new_down, preferred_element_type=jnp.float32) * out_scale
    retained = scatter_tokens(partial, local_rows).astype(jnp.bfloat16)
    return (retained, new_gate, new_up, new_down)


def solution(mesh):
    dp_size, mp_size = mesh.devices.shape
    physical = Mesh(mesh.devices.reshape(dp_size // 8, 2, 4, mp_size // 2, 2), DP + MP)
    rows = P(DP, MP)
    cols = P(MP, DP)
    in_specs = (rows, rows, rows, cols, cols, rows)
    out_specs = (rows, cols, cols, rows)
    return jax.shard_map(body, mesh=physical, in_specs=in_specs, out_specs=out_specs, check_vma=False)
```

```python
import math

import jax
import jax.numpy as jnp
from jax import lax
from jax.sharding import Mesh
from jax.sharding import PartitionSpec as P

D = 8192
FF = 16384


STEP_SIZE = 0.5

DP = ("x", "zh", "y")
MP = ("zl", "c")


def shift(v, axis, n, k):
    return lax.ppermute(v, axis, [(i, (i + k) % n) for i in range(n)])


def gather_ring(blocks, axis, n):
    if n == 2:
        return jnp.stack([blocks, shift(blocks, axis, 2, 1)])
    half = blocks.shape[-1] // 2
    left = shift(blocks, axis, n, 1)
    right = shift(blocks, axis, n, -1)
    far = jnp.concatenate(
        [shift(left[..., :half], axis, n, 1), shift(right[..., half:], axis, n, -1)], axis=-1
    )
    return jnp.stack([blocks, left, far, right])


def scatter_ring(parts, axis, n):
    send = lambda v, k: shift(v, axis, n, k)
    if n == 2:
        return parts[0] + send(parts[1], 1)
    half = parts.shape[-1] // 2
    near = parts[1].at[..., :half].add(send(parts[2][..., :half], -1))
    back = parts[3].at[..., half:].add(send(parts[2][..., half:], 1))
    return parts[0] + send(near, -1) + send(back, 1)


def gather_tokens(rows):
    half = rows.shape[1] // 2
    first = gather_ring(gather_ring(gather_ring(rows[:, :half], "zh", 2), "y", 4), "x", 4)
    second = gather_ring(gather_ring(gather_ring(rows[:, half:], "zh", 2), "x", 4), "y", 4)
    second = jnp.swapaxes(second, 0, 1)
    whole = jnp.concatenate([first, second], axis=-1)
    return whole.reshape(-1, rows.shape[1])


def scatter_tokens(sums, t):
    half = sums.shape[1] // 2
    parts = sums.reshape(4, 4, 2, t, sums.shape[1])
    first = scatter_ring(scatter_ring(scatter_ring(parts[..., :half], "x", 4), "y", 4), "zh", 2)
    second = jnp.swapaxes(parts[..., half:], 0, 1)
    second = scatter_ring(scatter_ring(scatter_ring(second, "y", 4), "x", 4), "zh", 2)
    return jnp.concatenate([first, second], axis=-1)


def gather_units(values):
    zl = lax.axis_index("zl")
    right, left, got_right, got_left = values, values, [], []
    for step in range(1, 4):
        right = lax.ppermute(right, "zl", [(k, k + 1) for k in range(step - 1, 3)])
        left = lax.ppermute(left, "zl", [(k, k - 1) for k in range(1, 5 - step)])
        got_right.append(right)
        got_left.append(left)
    line = jnp.stack(got_right[::-1] + [values] + got_left)
    blocks = lax.dynamic_slice_in_dim(line, 3 - zl, 4, axis=0)
    other = lax.ppermute(blocks, "c", [(0, 1), (1, 0)])
    first = lax.axis_index("c") == 0
    whole = jnp.where(first, jnp.stack([blocks, other], 1), jnp.stack([other, blocks], 1))
    return whole.reshape(-1, values.shape[1])


def scatter_units(sums):
    t = sums.shape[0] // 8
    parts = sums.reshape(4, 2, t, sums.shape[1])
    core = lax.axis_index("c")
    mine = lax.dynamic_index_in_dim(parts, core, axis=1, keepdims=False)
    other = lax.dynamic_index_in_dim(parts, 1 - core, axis=1, keepdims=False)
    send = lax.ppermute
    chip = mine + send(other, "c", [(0, 1), (1, 0)])
    zl = lax.axis_index("zl")
    pick = lambda b: lax.dynamic_index_in_dim(chip, jnp.clip(b, 0, 3), axis=0, keepdims=False)
    from_left = jnp.zeros_like(chip[0])
    from_right = jnp.zeros_like(chip[0])
    for step in range(1, 4):
        to_right = pick(4 + zl - step) + from_left
        to_left = pick(zl + step - 4) + from_right
        from_left = send(to_right, "zl", [(k, k + 1) for k in range(step)])
        from_right = send(to_left, "zl", [(k, k - 1) for k in range(4 - step, 4)])
    return pick(zl) + from_left + from_right


def scatter_units_direct(sums):
    t = sums.shape[0] // 8
    parts = sums.reshape(4, 2, t, sums.shape[1])
    core = lax.axis_index("c")
    mine = lax.dynamic_index_in_dim(parts, core, axis=1, keepdims=False)
    other = lax.dynamic_index_in_dim(parts, 1 - core, axis=1, keepdims=False)
    send = lambda v, axis, pairs: lax.ppermute(v.astype(jnp.bfloat16), axis, pairs).astype(jnp.float32)
    chip = mine + send(other, "c", [(0, 1), (1, 0)])
    zl = lax.axis_index("zl")
    total = lax.dynamic_index_in_dim(chip, zl, axis=0, keepdims=False)
    for k in range(1, 4):
        block = lax.dynamic_index_in_dim(chip, (zl + k) % 4, axis=0, keepdims=False)
        total = total + send(block, "zl", [(i, (i + k) % 4) for i in range(4)])
    return total


def project_sum(rows_all, weight_pair):
    width_scale = 1.0 / math.sqrt(D)
    return scatter_units(
        jnp.dot(rows_all, weight_pair, preferred_element_type=jnp.float32) * width_scale
    )


def activate(sums, unit_count):
    gate_sum = sums[:, :unit_count]
    up_sum = sums[:, unit_count:]
    sigmoid_gate = jax.nn.sigmoid(gate_sum)
    return (gate_sum, up_sum, sigmoid_gate, gate_sum * sigmoid_gate)


def unit_grads(back_units, gate_sum, up_sum, sigmoid_gate, active):
    grad_gate = back_units * up_sum * sigmoid_gate * (1.0 + gate_sum * (1.0 - sigmoid_gate))
    grad_up = back_units * active
    return jnp.concatenate([grad_gate, grad_up], axis=1).astype(jnp.bfloat16)


def body(forget_rows, cotangent, retain_rows, w_gate, w_up, w_down):
    unit_count = w_gate.shape[1]
    local_rows, width = forget_rows.shape
    width_scale = 1.0 / math.sqrt(D)
    contract_rows = (((0,), (0,)), ((), ()))
    contract_cols = (((1,), (1,)), ((), ()))
    gathered = gather_tokens(jnp.concatenate([forget_rows, cotangent], axis=1))
    forget_all = gathered[:, :width]
    cotan_all = gathered[:, width:]
    retain_all = gather_tokens(retain_rows)
    total_rows = forget_all.shape[0]
    token_scale = 1.0 / math.sqrt(total_rows)
    weight_pair = jnp.concatenate([w_gate, w_up], axis=1)
    forward = jnp.dot(forget_all, weight_pair, preferred_element_type=jnp.float32)
    backward = lax.dot_general(cotan_all, w_down, contract_cols, preferred_element_type=jnp.float32)
    both = scatter_units_direct(jnp.concatenate([forward, backward], axis=1) * width_scale)
    gate_sum, up_sum, sigmoid_gate, active = activate(both[:, : 2 * unit_count], unit_count)
    back_units = both[:, 2 * unit_count :]
    hidden = (active * up_sum).astype(jnp.bfloat16)
    units_all = gather_units(
        jnp.concatenate([hidden, unit_grads(back_units, gate_sum, up_sum, sigmoid_gate, active)], axis=1)
    )
    hidden_all = units_all[:, :unit_count]
    grads_all = units_all[:, unit_count:]
    grad_down = (
        lax.dot_general(hidden_all, cotan_all, contract_rows, preferred_element_type=jnp.float32)
        * token_scale
    )
    grad_pair = (
        lax.dot_general(forget_all, grads_all, contract_rows, preferred_element_type=jnp.float32)
        * token_scale
    )
    new_gate = (w_gate.astype(jnp.float32) + STEP_SIZE * grad_pair[:, :unit_count]).astype(
        jnp.bfloat16
    )
    new_up = (w_up.astype(jnp.float32) + STEP_SIZE * grad_pair[:, unit_count:]).astype(jnp.bfloat16)
    new_down = (w_down.astype(jnp.float32) + STEP_SIZE * grad_down).astype(jnp.bfloat16)
    new_pair = jnp.concatenate([new_gate, new_up], axis=1)
    keep_sums = project_sum(retain_all, new_pair)
    gate_keep, up_keep, sigmoid_keep, active_keep = activate(keep_sums, unit_count)
    hidden_keep = (active_keep * up_keep).astype(jnp.bfloat16)
    hidden_keep_all = gather_units(hidden_keep)
    out_scale = 1.0 / math.sqrt(FF)
    partial = jnp.dot(hidden_keep_all, new_down, preferred_element_type=jnp.float32) * out_scale
    retained = scatter_tokens(partial, local_rows).astype(jnp.bfloat16)
    return (retained, new_gate, new_up, new_down)


def solution(mesh):
    dp_size, mp_size = mesh.devices.shape
    physical = Mesh(mesh.devices.reshape(dp_size // 8, 2, 4, mp_size // 2, 2), DP + MP)
    rows = P(DP, MP)
    cols = P(MP, DP)
    in_specs = (rows, rows, rows, cols, cols, rows)
    out_specs = (rows, cols, cols, rows)
    return jax.shard_map(body, mesh=physical, in_specs=in_specs, out_specs=out_specs, check_vma=False)
```

```python
import math

import jax
import jax.numpy as jnp
from jax import lax
from jax.sharding import Mesh
from jax.sharding import PartitionSpec as P

D = 8192
FF = 16384


STEP_SIZE = 0.5

DP = ("x", "zh", "y")
MP = ("zl", "c")


def shift(v, axis, n, k):
    return lax.ppermute(v, axis, [(i, (i + k) % n) for i in range(n)])


def gather_ring(blocks, axis, n):
    if n == 2:
        return jnp.stack([blocks, shift(blocks, axis, 2, 1)])
    half = blocks.shape[-1] // 2
    left = shift(blocks, axis, n, 1)
    right = shift(blocks, axis, n, -1)
    far = jnp.concatenate(
        [shift(left[..., :half], axis, n, 1), shift(right[..., half:], axis, n, -1)], axis=-1
    )
    return jnp.stack([blocks, left, far, right])


def scatter_ring(parts, axis, n):
    send = lambda v, k: shift(v.astype(jnp.bfloat16), axis, n, k).astype(jnp.float32)
    if n == 2:
        return parts[0] + send(parts[1], 1)
    half = parts.shape[-1] // 2
    near = parts[1].at[..., :half].add(send(parts[2][..., :half], -1))
    back = parts[3].at[..., half:].add(send(parts[2][..., half:], 1))
    return parts[0] + send(near, -1) + send(back, 1)


def gather_tokens(rows):
    half = rows.shape[1] // 2
    first = gather_ring(gather_ring(gather_ring(rows[:, :half], "zh", 2), "y", 4), "x", 4)
    second = gather_ring(gather_ring(gather_ring(rows[:, half:], "zh", 2), "x", 4), "y", 4)
    second = jnp.swapaxes(second, 0, 1)
    whole = jnp.concatenate([first, second], axis=-1)
    return whole.reshape(-1, rows.shape[1])


def scatter_tokens(sums, t):
    half = sums.shape[1] // 2
    parts = sums.reshape(4, 4, 2, t, sums.shape[1])
    first = scatter_ring(scatter_ring(scatter_ring(parts[..., :half], "x", 4), "y", 4), "zh", 2)
    second = jnp.swapaxes(parts[..., half:], 0, 1)
    second = scatter_ring(scatter_ring(scatter_ring(second, "y", 4), "x", 4), "zh", 2)
    return jnp.concatenate([first, second], axis=-1)


def gather_units(values):
    zl = lax.axis_index("zl")
    got = [values] + [lax.ppermute(values, "zl", [(i, (i + k) % 4) for i in range(4)]) for k in range(1, 4)]
    blocks = jnp.take(jnp.stack(got), (zl - jnp.arange(4)) % 4, axis=0)
    other = lax.ppermute(blocks, "c", [(0, 1), (1, 0)])
    first = lax.axis_index("c") == 0
    whole = jnp.where(first, jnp.stack([blocks, other], 1), jnp.stack([other, blocks], 1))
    return whole.reshape(-1, values.shape[1])


def scatter_units(sums):
    t = sums.shape[0] // 8
    parts = sums.reshape(4, 2, t, sums.shape[1])
    core = lax.axis_index("c")
    mine = lax.dynamic_index_in_dim(parts, core, axis=1, keepdims=False)
    other = lax.dynamic_index_in_dim(parts, 1 - core, axis=1, keepdims=False)
    chip = mine + lax.ppermute(other, "c", [(0, 1), (1, 0)])
    zl = lax.axis_index("zl")
    total = lax.dynamic_index_in_dim(chip, zl, axis=0, keepdims=False)
    for k in range(1, 4):
        block = lax.dynamic_index_in_dim(chip, (zl + k) % 4, axis=0, keepdims=False)
        total = total + lax.ppermute(block, "zl", [(i, (i + k) % 4) for i in range(4)])
    return total


def project_sum(rows_all, weight_pair):
    width_scale = 1.0 / math.sqrt(D)
    return scatter_units(
        jnp.dot(rows_all, weight_pair, preferred_element_type=jnp.float32) * width_scale
    )


def activate(sums, unit_count):
    gate_sum = sums[:, :unit_count]
    up_sum = sums[:, unit_count:]
    sigmoid_gate = jax.nn.sigmoid(gate_sum)
    return (gate_sum, up_sum, sigmoid_gate, gate_sum * sigmoid_gate)


def unit_grads(back_units, gate_sum, up_sum, sigmoid_gate, active):
    grad_gate = back_units * up_sum * sigmoid_gate * (1.0 + gate_sum * (1.0 - sigmoid_gate))
    grad_up = back_units * active
    return jnp.concatenate([grad_gate, grad_up], axis=1).astype(jnp.bfloat16)


def body(forget_rows, cotangent, retain_rows, w_gate, w_up, w_down):
    unit_count = w_gate.shape[1]
    local_rows, width = forget_rows.shape
    width_scale = 1.0 / math.sqrt(D)
    contract_rows = (((0,), (0,)), ((), ()))
    contract_cols = (((1,), (1,)), ((), ()))
    gathered = gather_tokens(jnp.concatenate([forget_rows, cotangent, retain_rows], axis=1))
    forget_all = gathered[:, :width]
    cotan_all = gathered[:, width : 2 * width]
    retain_all = gathered[:, 2 * width :]
    total_rows = forget_all.shape[0]
    token_scale = 1.0 / math.sqrt(total_rows)
    weight_pair = jnp.concatenate([w_gate, w_up], axis=1)
    sums = project_sum(forget_all, weight_pair)
    gate_sum, up_sum, sigmoid_gate, active = activate(sums, unit_count)
    hidden = (active * up_sum).astype(jnp.bfloat16)
    hidden_all = gather_units(hidden)
    back_units = scatter_units(
        lax.dot_general(cotan_all, w_down, contract_cols, preferred_element_type=jnp.float32)
        * width_scale
    )
    grads_all = gather_units(unit_grads(back_units, gate_sum, up_sum, sigmoid_gate, active))
    grad_down = (
        lax.dot_general(hidden_all, cotan_all, contract_rows, preferred_element_type=jnp.float32)
        * token_scale
    )
    grad_pair = (
        lax.dot_general(forget_all, grads_all, contract_rows, preferred_element_type=jnp.float32)
        * token_scale
    )
    new_gate = (w_gate.astype(jnp.float32) + STEP_SIZE * grad_pair[:, :unit_count]).astype(
        jnp.bfloat16
    )
    new_up = (w_up.astype(jnp.float32) + STEP_SIZE * grad_pair[:, unit_count:]).astype(jnp.bfloat16)
    new_down = (w_down.astype(jnp.float32) + STEP_SIZE * grad_down).astype(jnp.bfloat16)
    new_pair = jnp.concatenate([new_gate, new_up], axis=1)
    keep_sums = project_sum(retain_all, new_pair)
    gate_keep, up_keep, sigmoid_keep, active_keep = activate(keep_sums, unit_count)
    hidden_keep = (active_keep * up_keep).astype(jnp.bfloat16)
    hidden_keep_all = gather_units(hidden_keep)
    out_scale = 1.0 / math.sqrt(FF)
    partial = jnp.dot(hidden_keep_all, new_down, preferred_element_type=jnp.float32) * out_scale
    retained = scatter_tokens(partial, local_rows).astype(jnp.bfloat16)
    return (retained, new_gate, new_up, new_down)


def solution(mesh):
    dp_size, mp_size = mesh.devices.shape
    physical = Mesh(mesh.devices.reshape(dp_size // 8, 2, 4, mp_size // 2, 2), DP + MP)
    rows = P(DP, MP)
    cols = P(MP, DP)
    in_specs = (rows, rows, rows, cols, cols, rows)
    out_specs = (rows, cols, cols, rows)
    return jax.shard_map(body, mesh=physical, in_specs=in_specs, out_specs=out_specs, check_vma=False)
```

```python
import math

import jax
import jax.numpy as jnp
from jax import lax
from jax.sharding import Mesh
from jax.sharding import PartitionSpec as P

D = 8192
FF = 16384


STEP_SIZE = 0.5

DP = ("x", "zh", "y")
MP = ("zl", "c")


def shift(v, axis, n, k):
    return lax.ppermute(v, axis, [(i, (i + k) % n) for i in range(n)])


def gather_ring(blocks, axis, n, direct=False):
    if direct:
        return jnp.stack([blocks] + [shift(blocks, axis, n, k) for k in range(1, n)])
    if n == 2:
        return jnp.stack([blocks, shift(blocks, axis, 2, 1)])
    half = blocks.shape[-1] // 2
    left = shift(blocks, axis, n, 1)
    right = shift(blocks, axis, n, -1)
    far = jnp.concatenate(
        [shift(left[..., :half], axis, n, 1), shift(right[..., half:], axis, n, -1)], axis=-1
    )
    return jnp.stack([blocks, left, far, right])


def scatter_ring(parts, axis, n, direct=False):
    send = lambda v, k: shift(v.astype(jnp.bfloat16), axis, n, k).astype(jnp.float32)
    if direct:
        return parts[0] + sum(send(parts[k], -k) for k in range(1, n))
    if n == 2:
        return parts[0] + send(parts[1], 1)
    half = parts.shape[-1] // 2
    near = parts[1].at[..., :half].add(send(parts[2][..., :half], -1))
    back = parts[3].at[..., half:].add(send(parts[2][..., half:], 1))
    return parts[0] + send(near, -1) + send(back, 1)


def gather_tokens(rows):
    half = rows.shape[1] // 2
    first = gather_ring(gather_ring(gather_ring(rows[:, :half], "zh", 2), "y", 4, True), "x", 4)
    second = gather_ring(gather_ring(gather_ring(rows[:, half:], "zh", 2), "x", 4, True), "y", 4)
    second = jnp.swapaxes(second, 0, 1)
    whole = jnp.concatenate([first, second], axis=-1)
    return whole.reshape(-1, rows.shape[1])


def scatter_tokens(sums, t):
    half = sums.shape[1] // 2
    parts = sums.reshape(4, 4, 2, t, sums.shape[1])
    first = scatter_ring(scatter_ring(scatter_ring(parts[..., :half], "x", 4), "y", 4, True), "zh", 2)
    second = jnp.swapaxes(parts[..., half:], 0, 1)
    second = scatter_ring(scatter_ring(scatter_ring(second, "y", 4), "x", 4, True), "zh", 2)
    return jnp.concatenate([first, second], axis=-1)


def gather_units(values):
    zl = lax.axis_index("zl")
    got = [values] + [lax.ppermute(values, "zl", [(i, (i + k) % 4) for i in range(4)]) for k in range(1, 4)]
    blocks = jnp.take(jnp.stack(got), (zl - jnp.arange(4)) % 4, axis=0)
    other = lax.ppermute(blocks, "c", [(0, 1), (1, 0)])
    first = lax.axis_index("c") == 0
    whole = jnp.where(first, jnp.stack([blocks, other], 1), jnp.stack([other, blocks], 1))
    return whole.reshape(-1, values.shape[1])


def scatter_units(sums):
    t = sums.shape[0] // 8
    parts = sums.reshape(4, 2, t, sums.shape[1])
    core = lax.axis_index("c")
    mine = lax.dynamic_index_in_dim(parts, core, axis=1, keepdims=False)
    other = lax.dynamic_index_in_dim(parts, 1 - core, axis=1, keepdims=False)
    chip = mine + lax.ppermute(other, "c", [(0, 1), (1, 0)])
    zl = lax.axis_index("zl")
    total = lax.dynamic_index_in_dim(chip, zl, axis=0, keepdims=False)
    for k in range(1, 4):
        block = lax.dynamic_index_in_dim(chip, (zl + k) % 4, axis=0, keepdims=False)
        total = total + lax.ppermute(block, "zl", [(i, (i + k) % 4) for i in range(4)])
    return total


def project_sum(rows_all, weight_pair):
    width_scale = 1.0 / math.sqrt(D)
    return scatter_units(
        jnp.dot(rows_all, weight_pair, preferred_element_type=jnp.float32) * width_scale
    )


def activate(sums, unit_count):
    gate_sum = sums[:, :unit_count]
    up_sum = sums[:, unit_count:]
    sigmoid_gate = jax.nn.sigmoid(gate_sum)
    return (gate_sum, up_sum, sigmoid_gate, gate_sum * sigmoid_gate)


def unit_grads(back_units, gate_sum, up_sum, sigmoid_gate, active):
    grad_gate = back_units * up_sum * sigmoid_gate * (1.0 + gate_sum * (1.0 - sigmoid_gate))
    grad_up = back_units * active
    return jnp.concatenate([grad_gate, grad_up], axis=1).astype(jnp.bfloat16)


def body(forget_rows, cotangent, retain_rows, w_gate, w_up, w_down):
    unit_count = w_gate.shape[1]
    local_rows, width = forget_rows.shape
    width_scale = 1.0 / math.sqrt(D)
    contract_rows = (((0,), (0,)), ((), ()))
    contract_cols = (((1,), (1,)), ((), ()))
    gathered = gather_tokens(jnp.concatenate([forget_rows, cotangent, retain_rows], axis=1))
    forget_all = gathered[:, :width]
    cotan_all = gathered[:, width : 2 * width]
    retain_all = gathered[:, 2 * width :]
    total_rows = forget_all.shape[0]
    token_scale = 1.0 / math.sqrt(total_rows)
    weight_pair = jnp.concatenate([w_gate, w_up], axis=1)
    sums = project_sum(forget_all, weight_pair)
    gate_sum, up_sum, sigmoid_gate, active = activate(sums, unit_count)
    hidden = (active * up_sum).astype(jnp.bfloat16)
    hidden_all = gather_units(hidden)
    back_units = scatter_units(
        lax.dot_general(cotan_all, w_down, contract_cols, preferred_element_type=jnp.float32)
        * width_scale
    )
    grads_all = gather_units(unit_grads(back_units, gate_sum, up_sum, sigmoid_gate, active))
    grad_down = (
        lax.dot_general(hidden_all, cotan_all, contract_rows, preferred_element_type=jnp.float32)
        * token_scale
    )
    grad_pair = (
        lax.dot_general(forget_all, grads_all, contract_rows, preferred_element_type=jnp.float32)
        * token_scale
    )
    new_gate = (w_gate.astype(jnp.float32) + STEP_SIZE * grad_pair[:, :unit_count]).astype(
        jnp.bfloat16
    )
    new_up = (w_up.astype(jnp.float32) + STEP_SIZE * grad_pair[:, unit_count:]).astype(jnp.bfloat16)
    new_down = (w_down.astype(jnp.float32) + STEP_SIZE * grad_down).astype(jnp.bfloat16)
    new_pair = jnp.concatenate([new_gate, new_up], axis=1)
    keep_sums = project_sum(retain_all, new_pair)
    gate_keep, up_keep, sigmoid_keep, active_keep = activate(keep_sums, unit_count)
    hidden_keep = (active_keep * up_keep).astype(jnp.bfloat16)
    hidden_keep_all = gather_units(hidden_keep)
    out_scale = 1.0 / math.sqrt(FF)
    partial = jnp.dot(hidden_keep_all, new_down, preferred_element_type=jnp.float32) * out_scale
    retained = scatter_tokens(partial, local_rows).astype(jnp.bfloat16)
    return (retained, new_gate, new_up, new_down)


def solution(mesh):
    dp_size, mp_size = mesh.devices.shape
    physical = Mesh(mesh.devices.reshape(dp_size // 8, 2, 4, mp_size // 2, 2), DP + MP)
    rows = P(DP, MP)
    cols = P(MP, DP)
    in_specs = (rows, rows, rows, cols, cols, rows)
    out_specs = (rows, cols, cols, rows)
    return jax.shard_map(body, mesh=physical, in_specs=in_specs, out_specs=out_specs, check_vma=False)
```

```python
import math

import jax
import jax.numpy as jnp
from jax import lax
from jax.sharding import Mesh
from jax.sharding import PartitionSpec as P

D = 8192
FF = 16384


STEP_SIZE = 0.5

DP = ("x", "zh", "y")
MP = ("zl", "c")


def shift(v, axis, n, k):
    return lax.ppermute(v, axis, [(i, (i + k) % n) for i in range(n)])


def gather_ring(blocks, axis, n, direct=False):
    if direct:
        return jnp.stack([blocks] + [shift(blocks, axis, n, k) for k in range(1, n)])
    if n == 2:
        return jnp.stack([blocks, shift(blocks, axis, 2, 1)])
    half = blocks.shape[-1] // 2
    left = shift(blocks, axis, n, 1)
    right = shift(blocks, axis, n, -1)
    far = jnp.concatenate(
        [shift(left[..., :half], axis, n, 1), shift(right[..., half:], axis, n, -1)], axis=-1
    )
    return jnp.stack([blocks, left, far, right])


def scatter_ring(parts, axis, n, direct=False):
    send = lambda v, k: shift(v.astype(jnp.bfloat16), axis, n, k).astype(jnp.float32)
    if direct:
        return parts[0] + sum(send(parts[k], -k) for k in range(1, n))
    if n == 2:
        return parts[0] + send(parts[1], 1)
    half = parts.shape[-1] // 2
    near = parts[1].at[..., :half].add(send(parts[2][..., :half], -1))
    back = parts[3].at[..., half:].add(send(parts[2][..., half:], 1))
    return parts[0] + send(near, -1) + send(back, 1)


def gather_tokens(rows):
    half = rows.shape[1] // 2
    first = gather_ring(gather_ring(gather_ring(rows[:, :half], "zh", 2), "y", 4, True), "x", 4)
    second = gather_ring(gather_ring(gather_ring(rows[:, half:], "zh", 2), "x", 4, True), "y", 4)
    second = jnp.swapaxes(second, 0, 1)
    whole = jnp.concatenate([first, second], axis=-1)
    return whole.reshape(-1, rows.shape[1])


def scatter_tokens(sums, t):
    half = sums.shape[1] // 2
    parts = sums.reshape(4, 4, 2, t, sums.shape[1])
    first = scatter_ring(scatter_ring(scatter_ring(parts[..., :half], "x", 4), "y", 4, True), "zh", 2)
    second = jnp.swapaxes(parts[..., half:], 0, 1)
    second = scatter_ring(scatter_ring(scatter_ring(second, "y", 4), "x", 4, True), "zh", 2)
    return jnp.concatenate([first, second], axis=-1)


def gather_units(values):
    zl = lax.axis_index("zl")
    got = [values] + [lax.ppermute(values, "zl", [(i, (i + k) % 4) for i in range(4)]) for k in range(1, 4)]
    blocks = jnp.take(jnp.stack(got), (zl - jnp.arange(4)) % 4, axis=0)
    other = lax.ppermute(blocks, "c", [(0, 1), (1, 0)])
    first = lax.axis_index("c") == 0
    whole = jnp.where(first, jnp.stack([blocks, other], 1), jnp.stack([other, blocks], 1))
    return whole.reshape(-1, values.shape[1])


def scatter_units(sums):
    t = sums.shape[0] // 8
    parts = sums.reshape(4, 2, t, sums.shape[1])
    core = lax.axis_index("c")
    mine = lax.dynamic_index_in_dim(parts, core, axis=1, keepdims=False)
    other = lax.dynamic_index_in_dim(parts, 1 - core, axis=1, keepdims=False)
    chip = mine + lax.ppermute(other, "c", [(0, 1), (1, 0)])
    zl = lax.axis_index("zl")
    total = lax.dynamic_index_in_dim(chip, zl, axis=0, keepdims=False)
    for k in range(1, 4):
        block = lax.dynamic_index_in_dim(chip, (zl + k) % 4, axis=0, keepdims=False)
        total = total + lax.ppermute(block, "zl", [(i, (i + k) % 4) for i in range(4)])
    return total


def project_sum(rows_all, weight_pair):
    width_scale = 1.0 / math.sqrt(D)
    return scatter_units(
        jnp.dot(rows_all, weight_pair, preferred_element_type=jnp.float32) * width_scale
    )


def activate(sums, unit_count):
    gate_sum = sums[:, :unit_count]
    up_sum = sums[:, unit_count:]
    sigmoid_gate = jax.nn.sigmoid(gate_sum)
    return (gate_sum, up_sum, sigmoid_gate, gate_sum * sigmoid_gate)


def unit_grads(back_units, gate_sum, up_sum, sigmoid_gate, active):
    grad_gate = back_units * up_sum * sigmoid_gate * (1.0 + gate_sum * (1.0 - sigmoid_gate))
    grad_up = back_units * active
    return jnp.concatenate([grad_gate, grad_up], axis=1).astype(jnp.bfloat16)


def body(forget_rows, cotangent, retain_rows, w_gate, w_up, w_down):
    unit_count = w_gate.shape[1]
    local_rows, width = forget_rows.shape
    width_scale = 1.0 / math.sqrt(D)
    contract_rows = (((0,), (0,)), ((), ()))
    contract_cols = (((1,), (1,)), ((), ()))
    gathered = gather_tokens(jnp.concatenate([forget_rows, cotangent], axis=1))
    forget_all = gathered[:, :width]
    cotan_all = gathered[:, width:]
    retain_all = gather_tokens(retain_rows)
    total_rows = forget_all.shape[0]
    token_scale = 1.0 / math.sqrt(total_rows)
    weight_pair = jnp.concatenate([w_gate, w_up], axis=1)
    sums = project_sum(forget_all, weight_pair)
    gate_sum, up_sum, sigmoid_gate, active = activate(sums, unit_count)
    hidden = (active * up_sum).astype(jnp.bfloat16)
    hidden_all = gather_units(hidden)
    back_units = scatter_units(
        lax.dot_general(cotan_all, w_down, contract_cols, preferred_element_type=jnp.float32)
        * width_scale
    )
    grads_all = gather_units(unit_grads(back_units, gate_sum, up_sum, sigmoid_gate, active))
    grad_down = (
        lax.dot_general(hidden_all, cotan_all, contract_rows, preferred_element_type=jnp.float32)
        * token_scale
    )
    grad_pair = (
        lax.dot_general(forget_all, grads_all, contract_rows, preferred_element_type=jnp.float32)
        * token_scale
    )
    new_gate = (w_gate.astype(jnp.float32) + STEP_SIZE * grad_pair[:, :unit_count]).astype(
        jnp.bfloat16
    )
    new_up = (w_up.astype(jnp.float32) + STEP_SIZE * grad_pair[:, unit_count:]).astype(jnp.bfloat16)
    new_down = (w_down.astype(jnp.float32) + STEP_SIZE * grad_down).astype(jnp.bfloat16)
    new_pair = jnp.concatenate([new_gate, new_up], axis=1)
    keep_sums = project_sum(retain_all, new_pair)
    gate_keep, up_keep, sigmoid_keep, active_keep = activate(keep_sums, unit_count)
    hidden_keep = (active_keep * up_keep).astype(jnp.bfloat16)
    hidden_keep_all = gather_units(hidden_keep)
    out_scale = 1.0 / math.sqrt(FF)
    partial = jnp.dot(hidden_keep_all, new_down, preferred_element_type=jnp.float32) * out_scale
    retained = scatter_tokens(partial, local_rows).astype(jnp.bfloat16)
    return (retained, new_gate, new_up, new_down)


def solution(mesh):
    dp_size, mp_size = mesh.devices.shape
    physical = Mesh(mesh.devices.reshape(dp_size // 8, 2, 4, mp_size // 2, 2), DP + MP)
    rows = P(DP, MP)
    cols = P(MP, DP)
    in_specs = (rows, rows, rows, cols, cols, rows)
    out_specs = (rows, cols, cols, rows)
    return jax.shard_map(body, mesh=physical, in_specs=in_specs, out_specs=out_specs, check_vma=False)
```

```python
import math

import jax
import jax.numpy as jnp
from jax import lax
from jax.sharding import Mesh
from jax.sharding import PartitionSpec as P

D = 8192
FF = 16384


STEP_SIZE = 0.5

DP = ("x", "zh", "y")
MP = ("zl", "c")


def shift(v, axis, n, k):
    return lax.ppermute(v, axis, [(i, (i + k) % n) for i in range(n)])


def gather_ring(blocks, axis, n, direct=False):
    if direct:
        return jnp.stack([blocks] + [shift(blocks, axis, n, k) for k in range(1, n)])
    if n == 2:
        return jnp.stack([blocks, shift(blocks, axis, 2, 1)])
    half = blocks.shape[-1] // 2
    left = shift(blocks, axis, n, 1)
    right = shift(blocks, axis, n, -1)
    far = jnp.concatenate(
        [shift(left[..., :half], axis, n, 1), shift(right[..., half:], axis, n, -1)], axis=-1
    )
    return jnp.stack([blocks, left, far, right])


def scatter_ring(parts, axis, n, direct=False):
    send = lambda v, k: shift(v.astype(jnp.bfloat16), axis, n, k).astype(jnp.float32)
    if direct:
        return parts[0] + sum(send(parts[k], -k) for k in range(1, n))
    if n == 2:
        return parts[0] + send(parts[1], 1)
    half = parts.shape[-1] // 2
    near = parts[1].at[..., :half].add(send(parts[2][..., :half], -1))
    back = parts[3].at[..., half:].add(send(parts[2][..., half:], 1))
    return parts[0] + send(near, -1) + send(back, 1)


def gather_tokens(rows):
    half = rows.shape[1] // 2
    first = gather_ring(gather_ring(gather_ring(rows[:, :half], "zh", 2), "y", 4, True), "x", 4)
    second = gather_ring(gather_ring(gather_ring(rows[:, half:], "zh", 2), "x", 4, True), "y", 4)
    second = jnp.swapaxes(second, 0, 1)
    whole = jnp.concatenate([first, second], axis=-1)
    return whole.reshape(-1, rows.shape[1])


def scatter_tokens_start(sums, t):
    half = sums.shape[1] // 2
    parts = sums.reshape(4, 4, 2, t, sums.shape[1])
    first = scatter_ring(parts[..., :half], "x", 4)
    second = scatter_ring(jnp.swapaxes(parts[..., half:], 0, 1), "y", 4)
    return first, second


def scatter_tokens_finish(first, second):
    first = scatter_ring(scatter_ring(first, "y", 4, True), "zh", 2)
    second = scatter_ring(scatter_ring(second, "x", 4, True), "zh", 2)
    return jnp.concatenate([first, second], axis=-1)


def gather_units(values):
    zl = lax.axis_index("zl")
    got = [values] + [lax.ppermute(values, "zl", [(i, (i + k) % 4) for i in range(4)]) for k in range(1, 4)]
    blocks = jnp.take(jnp.stack(got), (zl - jnp.arange(4)) % 4, axis=0)
    other = lax.ppermute(blocks, "c", [(0, 1), (1, 0)])
    first = lax.axis_index("c") == 0
    whole = jnp.where(first, jnp.stack([blocks, other], 1), jnp.stack([other, blocks], 1))
    return whole.reshape(-1, values.shape[1])


def scatter_units(sums):
    t = sums.shape[0] // 8
    parts = sums.reshape(4, 2, t, sums.shape[1])
    core = lax.axis_index("c")
    mine = lax.dynamic_index_in_dim(parts, core, axis=1, keepdims=False)
    other = lax.dynamic_index_in_dim(parts, 1 - core, axis=1, keepdims=False)
    chip = mine + lax.ppermute(other, "c", [(0, 1), (1, 0)])
    zl = lax.axis_index("zl")
    total = lax.dynamic_index_in_dim(chip, zl, axis=0, keepdims=False)
    for k in range(1, 4):
        block = lax.dynamic_index_in_dim(chip, (zl + k) % 4, axis=0, keepdims=False)
        total = total + lax.ppermute(block, "zl", [(i, (i + k) % 4) for i in range(4)])
    return total


def project_sum(rows_all, weight_pair):
    width_scale = 1.0 / math.sqrt(D)
    return scatter_units(
        jnp.dot(rows_all, weight_pair, preferred_element_type=jnp.float32) * width_scale
    )


def activate(sums, unit_count):
    gate_sum = sums[:, :unit_count]
    up_sum = sums[:, unit_count:]
    sigmoid_gate = jax.nn.sigmoid(gate_sum)
    return (gate_sum, up_sum, sigmoid_gate, gate_sum * sigmoid_gate)


def unit_grads(back_units, gate_sum, up_sum, sigmoid_gate, active):
    grad_gate = back_units * up_sum * sigmoid_gate * (1.0 + gate_sum * (1.0 - sigmoid_gate))
    grad_up = back_units * active
    return jnp.concatenate([grad_gate, grad_up], axis=1).astype(jnp.bfloat16)


def body(forget_rows, cotangent, retain_rows, w_gate, w_up, w_down):
    unit_count = w_gate.shape[1]
    local_rows, width = forget_rows.shape
    width_scale = 1.0 / math.sqrt(D)
    contract_rows = (((0,), (0,)), ((), ()))
    contract_cols = (((1,), (1,)), ((), ()))
    gathered = gather_tokens(jnp.concatenate([forget_rows, cotangent, retain_rows], axis=1))
    forget_all = gathered[:, :width]
    cotan_all = gathered[:, width : 2 * width]
    retain_all = gathered[:, 2 * width :]
    total_rows = forget_all.shape[0]
    token_scale = 1.0 / math.sqrt(total_rows)
    weight_pair = jnp.concatenate([w_gate, w_up], axis=1)
    sums = project_sum(forget_all, weight_pair)
    gate_sum, up_sum, sigmoid_gate, active = activate(sums, unit_count)
    hidden = (active * up_sum).astype(jnp.bfloat16)
    hidden_all = gather_units(hidden)
    back_units = scatter_units(
        lax.dot_general(cotan_all, w_down, contract_cols, preferred_element_type=jnp.float32)
        * width_scale
    )
    grads_all = gather_units(unit_grads(back_units, gate_sum, up_sum, sigmoid_gate, active))
    grad_down = (
        lax.dot_general(hidden_all, cotan_all, contract_rows, preferred_element_type=jnp.float32)
        * token_scale
    )
    grad_pair = (
        lax.dot_general(forget_all, grads_all, contract_rows, preferred_element_type=jnp.float32)
        * token_scale
    )
    new_gate = (w_gate.astype(jnp.float32) + STEP_SIZE * grad_pair[:, :unit_count]).astype(
        jnp.bfloat16
    )
    new_up = (w_up.astype(jnp.float32) + STEP_SIZE * grad_pair[:, unit_count:]).astype(jnp.bfloat16)
    new_down = (w_down.astype(jnp.float32) + STEP_SIZE * grad_down).astype(jnp.bfloat16)
    out_scale = 1.0 / math.sqrt(FF)
    half = unit_count // 2
    pairs = [
        jnp.concatenate([new_gate[:, units], new_up[:, units]], axis=1)
        for units in (slice(0, half), slice(half, unit_count))
    ]
    downs = [new_down[:half, :], new_down[half:, :]]
    started = []
    for part in range(2):
        keep_sums = project_sum(retain_all, pairs[part])
        gate_keep, up_keep, sigmoid_keep, active_keep = activate(keep_sums, half)
        hidden_keep = (active_keep * up_keep).astype(jnp.bfloat16)
        hidden_keep_all = gather_units(hidden_keep)
        partial = jnp.dot(hidden_keep_all, downs[part], preferred_element_type=jnp.float32) * out_scale
        started.append(scatter_tokens_start(partial, local_rows))
        if part == 0:
            started[0], pairs[1] = lax.optimization_barrier((started[0], pairs[1]))
    retained = scatter_tokens_finish(*started[0]) + scatter_tokens_finish(*started[1])
    retained = retained.astype(jnp.bfloat16)
    return (retained, new_gate, new_up, new_down)


def solution(mesh):
    dp_size, mp_size = mesh.devices.shape
    physical = Mesh(mesh.devices.reshape(dp_size // 8, 2, 4, mp_size // 2, 2), DP + MP)
    rows = P(DP, MP)
    cols = P(MP, DP)
    in_specs = (rows, rows, rows, cols, cols, rows)
    out_specs = (rows, cols, cols, rows)
    return jax.shard_map(body, mesh=physical, in_specs=in_specs, out_specs=out_specs, check_vma=False)
```

```python
import math

import jax
import jax.numpy as jnp
from jax import lax
from jax.sharding import Mesh
from jax.sharding import PartitionSpec as P

D = 8192
FF = 16384


STEP_SIZE = 0.5

DP = ("x", "zh", "y")
MP = ("zl", "c")


def shift(v, axis, n, k):
    return lax.ppermute(v, axis, [(i, (i + k) % n) for i in range(n)])


def gather_ring(blocks, axis, n, direct=False):
    if direct:
        return jnp.stack([blocks] + [shift(blocks, axis, n, k) for k in range(1, n)])
    if n == 2:
        return jnp.stack([blocks, shift(blocks, axis, 2, 1)])
    half = blocks.shape[-1] // 2
    left = shift(blocks, axis, n, 1)
    right = shift(blocks, axis, n, -1)
    far = jnp.concatenate(
        [shift(left[..., :half], axis, n, 1), shift(right[..., half:], axis, n, -1)], axis=-1
    )
    return jnp.stack([blocks, left, far, right])


def scatter_ring(parts, axis, n, direct=False):
    send = lambda v, k: shift(v.astype(jnp.bfloat16), axis, n, k).astype(jnp.float32)
    if direct:
        return parts[0] + sum(send(parts[k], -k) for k in range(1, n))
    if n == 2:
        return parts[0] + send(parts[1], 1)
    half = parts.shape[-1] // 2
    near = parts[1].at[..., :half].add(send(parts[2][..., :half], -1))
    back = parts[3].at[..., half:].add(send(parts[2][..., half:], 1))
    return parts[0] + send(near, -1) + send(back, 1)


def gather_tokens(rows):
    half = rows.shape[1] // 2
    first = gather_ring(gather_ring(gather_ring(rows[:, :half], "zh", 2), "y", 4, True), "x", 4)
    second = gather_ring(gather_ring(gather_ring(rows[:, half:], "zh", 2), "x", 4, True), "y", 4)
    second = jnp.swapaxes(second, 0, 1)
    whole = jnp.concatenate([first, second], axis=-1)
    return whole.reshape(-1, rows.shape[1])


def scatter_tokens(sums, t):
    half = sums.shape[1] // 2
    parts = sums.reshape(4, 4, 2, t, sums.shape[1])
    first = scatter_ring(scatter_ring(scatter_ring(parts[..., :half], "x", 4), "y", 4, True), "zh", 2)
    second = jnp.swapaxes(parts[..., half:], 0, 1)
    second = scatter_ring(scatter_ring(scatter_ring(second, "y", 4), "x", 4, True), "zh", 2)
    return jnp.concatenate([first, second], axis=-1)


def gather_units(values):
    zl = lax.axis_index("zl")
    got = [values] + [lax.ppermute(values, "zl", [(i, (i + k) % 4) for i in range(4)]) for k in range(1, 4)]
    blocks = jnp.take(jnp.stack(got), (zl - jnp.arange(4)) % 4, axis=0)
    other = lax.ppermute(blocks, "c", [(0, 1), (1, 0)])
    first = lax.axis_index("c") == 0
    whole = jnp.where(first, jnp.stack([blocks, other], 1), jnp.stack([other, blocks], 1))
    return whole.reshape(-1, values.shape[1])


def scatter_units(sums):
    t = sums.shape[0] // 8
    parts = sums.reshape(4, 2, t, sums.shape[1])
    core = lax.axis_index("c")
    mine = lax.dynamic_index_in_dim(parts, core, axis=1, keepdims=False)
    other = lax.dynamic_index_in_dim(parts, 1 - core, axis=1, keepdims=False)
    chip = mine + lax.ppermute(other, "c", [(0, 1), (1, 0)])
    zl = lax.axis_index("zl")
    total = lax.dynamic_index_in_dim(chip, zl, axis=0, keepdims=False)
    for k in range(1, 4):
        block = lax.dynamic_index_in_dim(chip, (zl + k) % 4, axis=0, keepdims=False)
        total = total + lax.ppermute(block, "zl", [(i, (i + k) % 4) for i in range(4)])
    return total


def project_sum(rows_all, weight_pair):
    width_scale = 1.0 / math.sqrt(D)
    return scatter_units(
        jnp.dot(rows_all, weight_pair, preferred_element_type=jnp.float32) * width_scale
    )


def activate(sums, unit_count):
    gate_sum = sums[:, :unit_count]
    up_sum = sums[:, unit_count:]
    sigmoid_gate = jax.nn.sigmoid(gate_sum)
    return (gate_sum, up_sum, sigmoid_gate, gate_sum * sigmoid_gate)


def unit_grads(back_units, gate_sum, up_sum, sigmoid_gate, active):
    grad_gate = back_units * up_sum * sigmoid_gate * (1.0 + gate_sum * (1.0 - sigmoid_gate))
    grad_up = back_units * active
    return jnp.concatenate([grad_gate, grad_up], axis=1).astype(jnp.bfloat16)


def body(forget_rows, cotangent, retain_rows, w_gate, w_up, w_down):
    unit_count = w_gate.shape[1]
    local_rows, width = forget_rows.shape
    width_scale = 1.0 / math.sqrt(D)
    contract_rows = (((0,), (0,)), ((), ()))
    contract_cols = (((1,), (1,)), ((), ()))
    gathered = gather_tokens(jnp.concatenate([forget_rows, cotangent, retain_rows], axis=1))
    forget_all = gathered[:, :width]
    cotan_all = gathered[:, width : 2 * width]
    retain_all = gathered[:, 2 * width :]
    total_rows = forget_all.shape[0]
    token_scale = 1.0 / math.sqrt(total_rows)
    weight_pair = jnp.concatenate([w_gate, w_up], axis=1)
    forward = jnp.dot(forget_all, weight_pair, preferred_element_type=jnp.float32)
    backward = lax.dot_general(cotan_all, w_down, contract_cols, preferred_element_type=jnp.float32)
    both = scatter_units(jnp.concatenate([forward, backward], axis=1) * width_scale)
    gate_sum, up_sum, sigmoid_gate, active = activate(both[:, : 2 * unit_count], unit_count)
    back_units = both[:, 2 * unit_count :]
    hidden = (active * up_sum).astype(jnp.bfloat16)
    units_all = gather_units(
        jnp.concatenate([hidden, unit_grads(back_units, gate_sum, up_sum, sigmoid_gate, active)], axis=1)
    )
    hidden_all = units_all[:, :unit_count]
    grads_all = units_all[:, unit_count:]
    grad_down = (
        lax.dot_general(hidden_all, cotan_all, contract_rows, preferred_element_type=jnp.float32)
        * token_scale
    )
    grad_pair = (
        lax.dot_general(forget_all, grads_all, contract_rows, preferred_element_type=jnp.float32)
        * token_scale
    )
    new_gate = (w_gate.astype(jnp.float32) + STEP_SIZE * grad_pair[:, :unit_count]).astype(
        jnp.bfloat16
    )
    new_up = (w_up.astype(jnp.float32) + STEP_SIZE * grad_pair[:, unit_count:]).astype(jnp.bfloat16)
    new_down = (w_down.astype(jnp.float32) + STEP_SIZE * grad_down).astype(jnp.bfloat16)
    new_pair = jnp.concatenate([new_gate, new_up], axis=1)
    keep_sums = project_sum(retain_all, new_pair)
    gate_keep, up_keep, sigmoid_keep, active_keep = activate(keep_sums, unit_count)
    hidden_keep = (active_keep * up_keep).astype(jnp.bfloat16)
    hidden_keep_all = gather_units(hidden_keep)
    out_scale = 1.0 / math.sqrt(FF)
    partial = jnp.dot(hidden_keep_all, new_down, preferred_element_type=jnp.float32) * out_scale
    retained = scatter_tokens(partial, local_rows).astype(jnp.bfloat16)
    return (retained, new_gate, new_up, new_down)


def solution(mesh):
    dp_size, mp_size = mesh.devices.shape
    physical = Mesh(mesh.devices.reshape(dp_size // 8, 2, 4, mp_size // 2, 2), DP + MP)
    rows = P(DP, MP)
    cols = P(MP, DP)
    in_specs = (rows, rows, rows, cols, cols, rows)
    out_specs = (rows, cols, cols, rows)
    return jax.shard_map(body, mesh=physical, in_specs=in_specs, out_specs=out_specs, check_vma=False)
```

```python
import math

import jax
import jax.numpy as jnp
from jax import lax
from jax.sharding import Mesh
from jax.sharding import PartitionSpec as P

D = 8192
FF = 16384


STEP_SIZE = 0.5

DP = ("x", "zh", "y")
MP = ("zl", "c")


def shift(v, axis, n, k):
    return lax.ppermute(v, axis, [(i, (i + k) % n) for i in range(n)])


def gather_ring(blocks, axis, n, direct=False):
    if direct:
        return jnp.stack([blocks] + [shift(blocks, axis, n, k) for k in range(1, n)])
    if n == 2:
        return jnp.stack([blocks, shift(blocks, axis, 2, 1)])
    half = blocks.shape[-1] // 2
    left = shift(blocks, axis, n, 1)
    right = shift(blocks, axis, n, -1)
    far = jnp.concatenate(
        [shift(left[..., :half], axis, n, 1), shift(right[..., half:], axis, n, -1)], axis=-1
    )
    return jnp.stack([blocks, left, far, right])


def scatter_ring(parts, axis, n, direct=False):
    send = lambda v, k: shift(v.astype(jnp.bfloat16), axis, n, k).astype(jnp.float32)
    if direct:
        return parts[0] + sum(send(parts[k], -k) for k in range(1, n))
    if n == 2:
        return parts[0] + send(parts[1], 1)
    half = parts.shape[-1] // 2
    near = parts[1].at[..., :half].add(send(parts[2][..., :half], -1))
    back = parts[3].at[..., half:].add(send(parts[2][..., half:], 1))
    return parts[0] + send(near, -1) + send(back, 1)


def gather_tokens(rows):
    half = rows.shape[1] // 2
    first = gather_ring(gather_ring(gather_ring(rows[:, :half], "zh", 2), "y", 4, True), "x", 4)
    second = gather_ring(gather_ring(gather_ring(rows[:, half:], "zh", 2), "x", 4, True), "y", 4)
    second = jnp.swapaxes(second, 0, 1)
    whole = jnp.concatenate([first, second], axis=-1)
    return whole.reshape(-1, rows.shape[1])


def scatter_tokens(sums, t):
    half = sums.shape[1] // 2
    parts = sums.reshape(4, 4, 2, t, sums.shape[1])
    first = scatter_ring(scatter_ring(scatter_ring(parts[..., :half], "x", 4), "y", 4, True), "zh", 2)
    second = jnp.swapaxes(parts[..., half:], 0, 1)
    second = scatter_ring(scatter_ring(scatter_ring(second, "y", 4), "x", 4, True), "zh", 2)
    return jnp.concatenate([first, second], axis=-1)


def gather_units(values):
    zl = lax.axis_index("zl")
    got = [values] + [lax.ppermute(values, "zl", [(i, (i + k) % 4) for i in range(4)]) for k in range(1, 4)]
    blocks = jnp.take(jnp.stack(got), (zl - jnp.arange(4)) % 4, axis=0)
    other = lax.ppermute(blocks, "c", [(0, 1), (1, 0)])
    first = lax.axis_index("c") == 0
    whole = jnp.where(first, jnp.stack([blocks, other], 1), jnp.stack([other, blocks], 1))
    return whole.reshape(-1, values.shape[1])


def scatter_units(sums, wire=None):
    t = sums.shape[0] // 8
    parts = sums.reshape(4, 2, t, sums.shape[1])
    core = lax.axis_index("c")
    mine = lax.dynamic_index_in_dim(parts, core, axis=1, keepdims=False)
    other = lax.dynamic_index_in_dim(parts, 1 - core, axis=1, keepdims=False)
    wire = wire or sums.dtype
    send = lambda v, axis, pairs: lax.ppermute(v.astype(wire), axis, pairs).astype(sums.dtype)
    chip = mine + send(other, "c", [(0, 1), (1, 0)])
    zl = lax.axis_index("zl")
    total = lax.dynamic_index_in_dim(chip, zl, axis=0, keepdims=False)
    for k in range(1, 4):
        block = lax.dynamic_index_in_dim(chip, (zl + k) % 4, axis=0, keepdims=False)
        total = total + send(block, "zl", [(i, (i + k) % 4) for i in range(4)])
    return total


def project_sum(rows_all, weight_pair):
    width_scale = 1.0 / math.sqrt(D)
    return scatter_units(
        jnp.dot(rows_all, weight_pair, preferred_element_type=jnp.float32) * width_scale
    )


def activate(sums, unit_count):
    gate_sum = sums[:, :unit_count]
    up_sum = sums[:, unit_count:]
    sigmoid_gate = jax.nn.sigmoid(gate_sum)
    return (gate_sum, up_sum, sigmoid_gate, gate_sum * sigmoid_gate)


def unit_grads(back_units, gate_sum, up_sum, sigmoid_gate, active):
    grad_gate = back_units * up_sum * sigmoid_gate * (1.0 + gate_sum * (1.0 - sigmoid_gate))
    grad_up = back_units * active
    return jnp.concatenate([grad_gate, grad_up], axis=1).astype(jnp.bfloat16)


def body(forget_rows, cotangent, retain_rows, w_gate, w_up, w_down):
    unit_count = w_gate.shape[1]
    local_rows, width = forget_rows.shape
    width_scale = 1.0 / math.sqrt(D)
    contract_rows = (((0,), (0,)), ((), ()))
    contract_cols = (((1,), (1,)), ((), ()))
    gathered = gather_tokens(jnp.concatenate([forget_rows, cotangent, retain_rows], axis=1))
    forget_all = gathered[:, :width]
    cotan_all = gathered[:, width : 2 * width]
    retain_all = gathered[:, 2 * width :]
    total_rows = forget_all.shape[0]
    token_scale = 1.0 / math.sqrt(total_rows)
    weight_pair = jnp.concatenate([w_gate, w_up], axis=1)
    sums = project_sum(forget_all, weight_pair)
    gate_sum, up_sum, sigmoid_gate, active = activate(sums, unit_count)
    hidden = (active * up_sum).astype(jnp.bfloat16)
    hidden_all = gather_units(hidden)
    back_units = scatter_units(
        lax.dot_general(cotan_all, w_down, contract_cols, preferred_element_type=jnp.float32)
        * width_scale,
        jnp.bfloat16,
    )
    grads_all = gather_units(unit_grads(back_units, gate_sum, up_sum, sigmoid_gate, active))
    grad_down = (
        lax.dot_general(hidden_all, cotan_all, contract_rows, preferred_element_type=jnp.float32)
        * token_scale
    )
    grad_pair = (
        lax.dot_general(forget_all, grads_all, contract_rows, preferred_element_type=jnp.float32)
        * token_scale
    )
    new_gate = (w_gate.astype(jnp.float32) + STEP_SIZE * grad_pair[:, :unit_count]).astype(
        jnp.bfloat16
    )
    new_up = (w_up.astype(jnp.float32) + STEP_SIZE * grad_pair[:, unit_count:]).astype(jnp.bfloat16)
    new_down = (w_down.astype(jnp.float32) + STEP_SIZE * grad_down).astype(jnp.bfloat16)
    new_pair = jnp.concatenate([new_gate, new_up], axis=1)
    keep_sums = project_sum(retain_all, new_pair)
    gate_keep, up_keep, sigmoid_keep, active_keep = activate(keep_sums, unit_count)
    hidden_keep = (active_keep * up_keep).astype(jnp.bfloat16)
    hidden_keep_all = gather_units(hidden_keep)
    out_scale = 1.0 / math.sqrt(FF)
    partial = jnp.dot(hidden_keep_all, new_down, preferred_element_type=jnp.float32) * out_scale
    retained = scatter_tokens(partial, local_rows).astype(jnp.bfloat16)
    return (retained, new_gate, new_up, new_down)


def solution(mesh):
    dp_size, mp_size = mesh.devices.shape
    physical = Mesh(mesh.devices.reshape(dp_size // 8, 2, 4, mp_size // 2, 2), DP + MP)
    rows = P(DP, MP)
    cols = P(MP, DP)
    in_specs = (rows, rows, rows, cols, cols, rows)
    out_specs = (rows, cols, cols, rows)
    return jax.shard_map(body, mesh=physical, in_specs=in_specs, out_specs=out_specs, check_vma=False)
```

```python
import math

import jax
import jax.numpy as jnp
from jax import lax
from jax.sharding import Mesh
from jax.sharding import PartitionSpec as P

D = 8192
FF = 16384


STEP_SIZE = 0.5

DP = ("x", "zh", "y")
MP = ("zl", "c")


def shift(v, axis, n, k):
    return lax.ppermute(v, axis, [(i, (i + k) % n) for i in range(n)])


def gather_ring(blocks, axis, n, direct=False):
    if direct:
        return jnp.stack([blocks] + [shift(blocks, axis, n, k) for k in range(1, n)])
    if n == 2:
        return jnp.stack([blocks, shift(blocks, axis, 2, 1)])
    half = blocks.shape[-1] // 2
    left = shift(blocks, axis, n, 1)
    right = shift(blocks, axis, n, -1)
    far = jnp.concatenate(
        [shift(left[..., :half], axis, n, 1), shift(right[..., half:], axis, n, -1)], axis=-1
    )
    return jnp.stack([blocks, left, far, right])


def scatter_ring(parts, axis, n, direct=False):
    send = lambda v, k: shift(v.astype(jnp.bfloat16), axis, n, k).astype(jnp.float32)
    if direct:
        return parts[0] + sum(send(parts[k], -k) for k in range(1, n))
    if n == 2:
        return parts[0] + send(parts[1], 1)
    half = parts.shape[-1] // 2
    near = parts[1].at[..., :half].add(send(parts[2][..., :half], -1))
    back = parts[3].at[..., half:].add(send(parts[2][..., half:], 1))
    return parts[0] + send(near, -1) + send(back, 1)


def gather_tokens(rows):
    half = rows.shape[1] // 2
    first = gather_ring(gather_ring(gather_ring(rows[:, :half], "zh", 2), "y", 4, True), "x", 4)
    second = gather_ring(gather_ring(gather_ring(rows[:, half:], "zh", 2), "x", 4, True), "y", 4)
    second = jnp.swapaxes(second, 0, 1)
    whole = jnp.concatenate([first, second], axis=-1)
    return whole.reshape(-1, rows.shape[1])


def scatter_tokens(sums, t):
    half = sums.shape[1] // 2
    parts = sums.reshape(4, 4, 2, t, sums.shape[1])
    first = scatter_ring(scatter_ring(scatter_ring(parts[..., :half], "x", 4), "y", 4, True), "zh", 2)
    second = jnp.swapaxes(parts[..., half:], 0, 1)
    second = scatter_ring(scatter_ring(scatter_ring(second, "y", 4), "x", 4, True), "zh", 2)
    return jnp.concatenate([first, second], axis=-1)


def gather_units(values):
    zl = lax.axis_index("zl")
    got = [values] + [lax.ppermute(values, "zl", [(i, (i + k) % 4) for i in range(4)]) for k in range(1, 4)]
    blocks = jnp.take(jnp.stack(got), (zl - jnp.arange(4)) % 4, axis=0)
    other = lax.ppermute(blocks, "c", [(0, 1), (1, 0)])
    first = lax.axis_index("c") == 0
    whole = jnp.where(first, jnp.stack([blocks, other], 1), jnp.stack([other, blocks], 1))
    return whole.reshape(-1, values.shape[1])


def scatter_units(sums, wire=None):
    t = sums.shape[0] // 8
    parts = sums.reshape(4, 2, t, sums.shape[1])
    core = lax.axis_index("c")
    mine = lax.dynamic_index_in_dim(parts, core, axis=1, keepdims=False)
    other = lax.dynamic_index_in_dim(parts, 1 - core, axis=1, keepdims=False)
    wire = wire or sums.dtype
    send = lambda v, axis, pairs: lax.ppermute(v.astype(wire), axis, pairs).astype(sums.dtype)
    chip = mine + send(other, "c", [(0, 1), (1, 0)])
    zl = lax.axis_index("zl")
    total = lax.dynamic_index_in_dim(chip, zl, axis=0, keepdims=False)
    for k in range(1, 4):
        block = lax.dynamic_index_in_dim(chip, (zl + k) % 4, axis=0, keepdims=False)
        total = total + send(block, "zl", [(i, (i + k) % 4) for i in range(4)])
    return total


def project_sum(rows_all, weight_pair):
    width_scale = 1.0 / math.sqrt(D)
    return scatter_units(
        jnp.dot(rows_all, weight_pair, preferred_element_type=jnp.float32) * width_scale
    )


def activate(sums, unit_count):
    gate_sum = sums[:, :unit_count]
    up_sum = sums[:, unit_count:]
    sigmoid_gate = jax.nn.sigmoid(gate_sum)
    return (gate_sum, up_sum, sigmoid_gate, gate_sum * sigmoid_gate)


def unit_grads(back_units, gate_sum, up_sum, sigmoid_gate, active):
    grad_gate = back_units * up_sum * sigmoid_gate * (1.0 + gate_sum * (1.0 - sigmoid_gate))
    grad_up = back_units * active
    return jnp.concatenate([grad_gate, grad_up], axis=1).astype(jnp.bfloat16)


def body(forget_rows, cotangent, retain_rows, w_gate, w_up, w_down):
    unit_count = w_gate.shape[1]
    local_rows, width = forget_rows.shape
    width_scale = 1.0 / math.sqrt(D)
    contract_rows = (((0,), (0,)), ((), ()))
    contract_cols = (((1,), (1,)), ((), ()))
    gathered = gather_tokens(jnp.concatenate([forget_rows, cotangent, retain_rows], axis=1))
    forget_all = gathered[:, :width]
    cotan_all = gathered[:, width : 2 * width]
    retain_all = gathered[:, 2 * width :]
    total_rows = forget_all.shape[0]
    token_scale = 1.0 / math.sqrt(total_rows)
    weight_pair = jnp.concatenate([w_gate, w_up], axis=1)
    sums = project_sum(forget_all, weight_pair)
    gate_sum, up_sum, sigmoid_gate, active = activate(sums, unit_count)
    hidden = (active * up_sum).astype(jnp.bfloat16)
    hidden_all = gather_units(hidden)
    back_units = scatter_units(
        lax.dot_general(cotan_all, w_down, contract_cols, preferred_element_type=jnp.float32)
        * width_scale,
        jnp.bfloat16,
    )
    grads_all = gather_units(unit_grads(back_units, gate_sum, up_sum, sigmoid_gate, active))
    grad_down = (
        lax.dot_general(hidden_all, cotan_all, contract_rows, preferred_element_type=jnp.float32)
        * token_scale
    )
    grad_pair = (
        lax.dot_general(forget_all, grads_all, contract_rows, preferred_element_type=jnp.float32)
        * token_scale
    )
    new_gate = (w_gate.astype(jnp.float32) + STEP_SIZE * grad_pair[:, :unit_count]).astype(
        jnp.bfloat16
    )
    new_up = (w_up.astype(jnp.float32) + STEP_SIZE * grad_pair[:, unit_count:]).astype(jnp.bfloat16)
    new_down = (w_down.astype(jnp.float32) + STEP_SIZE * grad_down).astype(jnp.bfloat16)
    new_pair = jnp.concatenate([new_gate, new_up], axis=1)
    new_pair, hidden_all = lax.optimization_barrier((new_pair, hidden_all))
    keep_sums = project_sum(retain_all, new_pair)
    gate_keep, up_keep, sigmoid_keep, active_keep = activate(keep_sums, unit_count)
    hidden_keep = (active_keep * up_keep).astype(jnp.bfloat16)
    hidden_keep_all = gather_units(hidden_keep)
    out_scale = 1.0 / math.sqrt(FF)
    partial = jnp.dot(hidden_keep_all, new_down, preferred_element_type=jnp.float32) * out_scale
    retained = scatter_tokens(partial, local_rows).astype(jnp.bfloat16)
    return (retained, new_gate, new_up, new_down)


def solution(mesh):
    dp_size, mp_size = mesh.devices.shape
    physical = Mesh(mesh.devices.reshape(dp_size // 8, 2, 4, mp_size // 2, 2), DP + MP)
    rows = P(DP, MP)
    cols = P(MP, DP)
    in_specs = (rows, rows, rows, cols, cols, rows)
    out_specs = (rows, cols, cols, rows)
    return jax.shard_map(body, mesh=physical, in_specs=in_specs, out_specs=out_specs, check_vma=False)
```

```python
import math

import jax
import jax.numpy as jnp
from jax import lax
from jax.sharding import Mesh
from jax.sharding import PartitionSpec as P

D = 8192
FF = 16384


STEP_SIZE = 0.5

DP = ("x", "zh", "y")
MP = ("zl", "c")


def shift(v, axis, n, k):
    return lax.ppermute(v, axis, [(i, (i + k) % n) for i in range(n)])


def gather_ring(blocks, axis, n, direct=False):
    if direct:
        return jnp.stack([blocks] + [shift(blocks, axis, n, k) for k in range(1, n)])
    if n == 2:
        return jnp.stack([blocks, shift(blocks, axis, 2, 1)])
    half = blocks.shape[-1] // 2
    left = shift(blocks, axis, n, 1)
    right = shift(blocks, axis, n, -1)
    far = jnp.concatenate(
        [shift(left[..., :half], axis, n, 1), shift(right[..., half:], axis, n, -1)], axis=-1
    )
    return jnp.stack([blocks, left, far, right])


def scatter_ring(parts, axis, n, direct=False):
    send = lambda v, k: shift(v.astype(jnp.bfloat16), axis, n, k).astype(jnp.float32)
    if direct:
        return parts[0] + sum(send(parts[k], -k) for k in range(1, n))
    if n == 2:
        return parts[0] + send(parts[1], 1)
    half = parts.shape[-1] // 2
    near = parts[1].at[..., :half].add(send(parts[2][..., :half], -1))
    back = parts[3].at[..., half:].add(send(parts[2][..., half:], 1))
    return parts[0] + send(near, -1) + send(back, 1)


def gather_tokens(rows):
    half = rows.shape[1] // 2
    first = gather_ring(gather_ring(gather_ring(rows[:, :half], "zh", 2), "y", 4, True), "x", 4)
    second = gather_ring(gather_ring(gather_ring(rows[:, half:], "zh", 2), "x", 4, True), "y", 4)
    second = jnp.swapaxes(second, 0, 1)
    whole = jnp.concatenate([first, second], axis=-1)
    return whole.reshape(-1, rows.shape[1])


def scatter_tokens(sums, t):
    half = sums.shape[1] // 2
    parts = sums.reshape(4, 4, 2, t, sums.shape[1])
    first = scatter_ring(scatter_ring(scatter_ring(parts[..., :half], "x", 4, True), "y", 4, True), "zh", 2)
    second = jnp.swapaxes(parts[..., half:], 0, 1)
    second = scatter_ring(scatter_ring(scatter_ring(second, "y", 4, True), "x", 4, True), "zh", 2)
    return jnp.concatenate([first, second], axis=-1)


def gather_units(values):
    zl = lax.axis_index("zl")
    got = [values] + [lax.ppermute(values, "zl", [(i, (i + k) % 4) for i in range(4)]) for k in range(1, 4)]
    blocks = jnp.take(jnp.stack(got), (zl - jnp.arange(4)) % 4, axis=0)
    other = lax.ppermute(blocks, "c", [(0, 1), (1, 0)])
    first = lax.axis_index("c") == 0
    whole = jnp.where(first, jnp.stack([blocks, other], 1), jnp.stack([other, blocks], 1))
    return whole.reshape(-1, values.shape[1])


def scatter_units(sums, wire=None):
    t = sums.shape[0] // 8
    parts = sums.reshape(4, 2, t, sums.shape[1])
    core = lax.axis_index("c")
    mine = lax.dynamic_index_in_dim(parts, core, axis=1, keepdims=False)
    other = lax.dynamic_index_in_dim(parts, 1 - core, axis=1, keepdims=False)
    wire = wire or sums.dtype
    send = lambda v, axis, pairs: lax.ppermute(v.astype(wire), axis, pairs).astype(sums.dtype)
    chip = mine + send(other, "c", [(0, 1), (1, 0)])
    zl = lax.axis_index("zl")
    total = lax.dynamic_index_in_dim(chip, zl, axis=0, keepdims=False)
    for k in range(1, 4):
        block = lax.dynamic_index_in_dim(chip, (zl + k) % 4, axis=0, keepdims=False)
        total = total + send(block, "zl", [(i, (i + k) % 4) for i in range(4)])
    return total


def project_sum(rows_all, weight_pair):
    width_scale = 1.0 / math.sqrt(D)
    return scatter_units(
        jnp.dot(rows_all, weight_pair, preferred_element_type=jnp.float32) * width_scale
    )


def activate(sums, unit_count):
    gate_sum = sums[:, :unit_count]
    up_sum = sums[:, unit_count:]
    sigmoid_gate = jax.nn.sigmoid(gate_sum)
    return (gate_sum, up_sum, sigmoid_gate, gate_sum * sigmoid_gate)


def unit_grads(back_units, gate_sum, up_sum, sigmoid_gate, active):
    grad_gate = back_units * up_sum * sigmoid_gate * (1.0 + gate_sum * (1.0 - sigmoid_gate))
    grad_up = back_units * active
    return jnp.concatenate([grad_gate, grad_up], axis=1).astype(jnp.bfloat16)


def body(forget_rows, cotangent, retain_rows, w_gate, w_up, w_down):
    unit_count = w_gate.shape[1]
    local_rows, width = forget_rows.shape
    width_scale = 1.0 / math.sqrt(D)
    contract_rows = (((0,), (0,)), ((), ()))
    contract_cols = (((1,), (1,)), ((), ()))
    gathered = gather_tokens(jnp.concatenate([forget_rows, cotangent, retain_rows], axis=1))
    forget_all = gathered[:, :width]
    cotan_all = gathered[:, width : 2 * width]
    retain_all = gathered[:, 2 * width :]
    total_rows = forget_all.shape[0]
    token_scale = 1.0 / math.sqrt(total_rows)
    weight_pair = jnp.concatenate([w_gate, w_up], axis=1)
    sums = project_sum(forget_all, weight_pair)
    gate_sum, up_sum, sigmoid_gate, active = activate(sums, unit_count)
    hidden = (active * up_sum).astype(jnp.bfloat16)
    hidden_all = gather_units(hidden)
    back_units = scatter_units(
        lax.dot_general(cotan_all, w_down, contract_cols, preferred_element_type=jnp.float32)
        * width_scale,
        jnp.bfloat16,
    )
    grads_all = gather_units(unit_grads(back_units, gate_sum, up_sum, sigmoid_gate, active))
    grad_down = (
        lax.dot_general(hidden_all, cotan_all, contract_rows, preferred_element_type=jnp.float32)
        * token_scale
    )
    grad_pair = (
        lax.dot_general(forget_all, grads_all, contract_rows, preferred_element_type=jnp.float32)
        * token_scale
    )
    new_gate = (w_gate.astype(jnp.float32) + STEP_SIZE * grad_pair[:, :unit_count]).astype(
        jnp.bfloat16
    )
    new_up = (w_up.astype(jnp.float32) + STEP_SIZE * grad_pair[:, unit_count:]).astype(jnp.bfloat16)
    new_down = (w_down.astype(jnp.float32) + STEP_SIZE * grad_down).astype(jnp.bfloat16)
    new_pair = jnp.concatenate([new_gate, new_up], axis=1)
    new_pair, hidden_all = lax.optimization_barrier((new_pair, hidden_all))
    keep_sums = project_sum(retain_all, new_pair)
    gate_keep, up_keep, sigmoid_keep, active_keep = activate(keep_sums, unit_count)
    hidden_keep = (active_keep * up_keep).astype(jnp.bfloat16)
    hidden_keep_all = gather_units(hidden_keep)
    out_scale = 1.0 / math.sqrt(FF)
    partial = jnp.dot(hidden_keep_all, new_down, preferred_element_type=jnp.float32) * out_scale
    retained = scatter_tokens(partial, local_rows).astype(jnp.bfloat16)
    return (retained, new_gate, new_up, new_down)


def solution(mesh):
    dp_size, mp_size = mesh.devices.shape
    physical = Mesh(mesh.devices.reshape(dp_size // 8, 2, 4, mp_size // 2, 2), DP + MP)
    rows = P(DP, MP)
    cols = P(MP, DP)
    in_specs = (rows, rows, rows, cols, cols, rows)
    out_specs = (rows, cols, cols, rows)
    return jax.shard_map(body, mesh=physical, in_specs=in_specs, out_specs=out_specs, check_vma=False)
```

```python
import math

import jax
import jax.numpy as jnp
from jax import lax
from jax.sharding import Mesh
from jax.sharding import PartitionSpec as P

D = 8192
FF = 16384


STEP_SIZE = 0.5

DP = ("x", "zh", "y")
MP = ("zl", "c")


def shift(v, axis, n, k):
    return lax.ppermute(v, axis, [(i, (i + k) % n) for i in range(n)])


def gather_ring(blocks, axis, n, direct=False):
    if direct:
        return jnp.stack([blocks] + [shift(blocks, axis, n, k) for k in range(1, n)])
    if n == 2:
        return jnp.stack([blocks, shift(blocks, axis, 2, 1)])
    half = blocks.shape[-1] // 2
    left = shift(blocks, axis, n, 1)
    right = shift(blocks, axis, n, -1)
    far = jnp.concatenate(
        [shift(left[..., :half], axis, n, 1), shift(right[..., half:], axis, n, -1)], axis=-1
    )
    return jnp.stack([blocks, left, far, right])


def scatter_ring(parts, axis, n, direct=False):
    send = lambda v, k: shift(v.astype(jnp.bfloat16), axis, n, k).astype(jnp.float32)
    if direct:
        return parts[0] + sum(send(parts[k], -k) for k in range(1, n))
    if n == 2:
        return parts[0] + send(parts[1], 1)
    half = parts.shape[-1] // 2
    near = parts[1].at[..., :half].add(send(parts[2][..., :half], -1))
    back = parts[3].at[..., half:].add(send(parts[2][..., half:], 1))
    return parts[0] + send(near, -1) + send(back, 1)


def gather_tokens(rows):
    half = rows.shape[1] // 2
    first = gather_ring(gather_ring(gather_ring(rows[:, :half], "zh", 2), "y", 4, True), "x", 4)
    second = gather_ring(gather_ring(gather_ring(rows[:, half:], "zh", 2), "x", 4, True), "y", 4)
    second = jnp.swapaxes(second, 0, 1)
    whole = jnp.concatenate([first, second], axis=-1)
    return whole.reshape(-1, rows.shape[1])


def scatter_tokens(sums, t):
    half = sums.shape[1] // 2
    parts = sums.reshape(4, 4, 2, t, sums.shape[1])
    first = scatter_ring(scatter_ring(scatter_ring(parts[..., :half], "x", 4), "y", 4, True), "zh", 2)
    second = jnp.swapaxes(parts[..., half:], 0, 1)
    second = scatter_ring(scatter_ring(scatter_ring(second, "y", 4), "x", 4, True), "zh", 2)
    return jnp.concatenate([first, second], axis=-1)


def gather_units(values):
    zl = lax.axis_index("zl")
    got = [values] + [lax.ppermute(values, "zl", [(i, (i + k) % 4) for i in range(4)]) for k in range(1, 4)]
    blocks = jnp.take(jnp.stack(got), (zl - jnp.arange(4)) % 4, axis=0)
    other = lax.ppermute(blocks, "c", [(0, 1), (1, 0)])
    first = lax.axis_index("c") == 0
    whole = jnp.where(first, jnp.stack([blocks, other], 1), jnp.stack([other, blocks], 1))
    return whole.reshape(-1, values.shape[1])


def scatter_units(sums, wire=None):
    t = sums.shape[0] // 8
    parts = sums.reshape(4, 2, t, sums.shape[1])
    core = lax.axis_index("c")
    mine = lax.dynamic_index_in_dim(parts, core, axis=1, keepdims=False)
    other = lax.dynamic_index_in_dim(parts, 1 - core, axis=1, keepdims=False)
    wire = wire or sums.dtype
    send = lambda v, axis, pairs: lax.ppermute(v.astype(wire), axis, pairs).astype(sums.dtype)
    chip = mine + send(other, "c", [(0, 1), (1, 0)])
    zl = lax.axis_index("zl")
    total = lax.dynamic_index_in_dim(chip, zl, axis=0, keepdims=False)
    for k in range(1, 4):
        block = lax.dynamic_index_in_dim(chip, (zl + k) % 4, axis=0, keepdims=False)
        total = total + send(block, "zl", [(i, (i + k) % 4) for i in range(4)])
    return total


def scatter_units_chain(sums):
    t = sums.shape[0] // 8
    parts = sums.reshape(4, 2, t, sums.shape[1])
    core = lax.axis_index("c")
    mine = lax.dynamic_index_in_dim(parts, core, axis=1, keepdims=False)
    other = lax.dynamic_index_in_dim(parts, 1 - core, axis=1, keepdims=False)
    chip = mine + lax.ppermute(other, "c", [(0, 1), (1, 0)])
    zl = lax.axis_index("zl")
    pick = lambda b: lax.dynamic_index_in_dim(chip, jnp.clip(b, 0, 3), axis=0, keepdims=False)
    from_left = jnp.zeros_like(chip[0])
    from_right = jnp.zeros_like(chip[0])
    for step in range(1, 4):
        to_right = pick(4 + zl - step) + from_left
        to_left = pick(zl + step - 4) + from_right
        from_left = lax.ppermute(to_right, "zl", [(k, k + 1) for k in range(step)])
        from_right = lax.ppermute(to_left, "zl", [(k, k - 1) for k in range(4 - step, 4)])
    return pick(zl) + from_left + from_right


def project_sum(rows_all, weight_pair):
    width_scale = 1.0 / math.sqrt(D)
    return scatter_units(
        jnp.dot(rows_all, weight_pair, preferred_element_type=jnp.float32) * width_scale
    )


def activate(sums, unit_count):
    gate_sum = sums[:, :unit_count]
    up_sum = sums[:, unit_count:]
    sigmoid_gate = jax.nn.sigmoid(gate_sum)
    return (gate_sum, up_sum, sigmoid_gate, gate_sum * sigmoid_gate)


def unit_grads(back_units, gate_sum, up_sum, sigmoid_gate, active):
    grad_gate = back_units * up_sum * sigmoid_gate * (1.0 + gate_sum * (1.0 - sigmoid_gate))
    grad_up = back_units * active
    return jnp.concatenate([grad_gate, grad_up], axis=1).astype(jnp.bfloat16)


def body(forget_rows, cotangent, retain_rows, w_gate, w_up, w_down):
    unit_count = w_gate.shape[1]
    local_rows, width = forget_rows.shape
    width_scale = 1.0 / math.sqrt(D)
    contract_rows = (((0,), (0,)), ((), ()))
    contract_cols = (((1,), (1,)), ((), ()))
    gathered = gather_tokens(jnp.concatenate([forget_rows, cotangent, retain_rows], axis=1))
    forget_all = gathered[:, :width]
    cotan_all = gathered[:, width : 2 * width]
    retain_all = gathered[:, 2 * width :]
    total_rows = forget_all.shape[0]
    token_scale = 1.0 / math.sqrt(total_rows)
    weight_pair = jnp.concatenate([w_gate, w_up], axis=1)
    sums = project_sum(forget_all, weight_pair)
    gate_sum, up_sum, sigmoid_gate, active = activate(sums, unit_count)
    hidden = (active * up_sum).astype(jnp.bfloat16)
    hidden_all = gather_units(hidden)
    back_units = scatter_units(
        lax.dot_general(cotan_all, w_down, contract_cols, preferred_element_type=jnp.float32)
        * width_scale,
        jnp.bfloat16,
    )
    grads_all = gather_units(unit_grads(back_units, gate_sum, up_sum, sigmoid_gate, active))
    grad_down = (
        lax.dot_general(hidden_all, cotan_all, contract_rows, preferred_element_type=jnp.float32)
        * token_scale
    )
    grad_pair = (
        lax.dot_general(forget_all, grads_all, contract_rows, preferred_element_type=jnp.float32)
        * token_scale
    )
    new_gate = (w_gate.astype(jnp.float32) + STEP_SIZE * grad_pair[:, :unit_count]).astype(
        jnp.bfloat16
    )
    new_up = (w_up.astype(jnp.float32) + STEP_SIZE * grad_pair[:, unit_count:]).astype(jnp.bfloat16)
    new_down = (w_down.astype(jnp.float32) + STEP_SIZE * grad_down).astype(jnp.bfloat16)
    new_pair = jnp.concatenate([new_gate, new_up], axis=1)
    new_pair, hidden_all = lax.optimization_barrier((new_pair, hidden_all))
    keep_sums = scatter_units_chain(
        jnp.dot(retain_all, new_pair, preferred_element_type=jnp.float32) * width_scale
    )
    gate_keep, up_keep, sigmoid_keep, active_keep = activate(keep_sums, unit_count)
    hidden_keep = (active_keep * up_keep).astype(jnp.bfloat16)
    hidden_keep_all = gather_units(hidden_keep)
    out_scale = 1.0 / math.sqrt(FF)
    partial = jnp.dot(hidden_keep_all, new_down, preferred_element_type=jnp.float32) * out_scale
    retained = scatter_tokens(partial, local_rows).astype(jnp.bfloat16)
    return (retained, new_gate, new_up, new_down)


def solution(mesh):
    dp_size, mp_size = mesh.devices.shape
    physical = Mesh(mesh.devices.reshape(dp_size // 8, 2, 4, mp_size // 2, 2), DP + MP)
    rows = P(DP, MP)
    cols = P(MP, DP)
    in_specs = (rows, rows, rows, cols, cols, rows)
    out_specs = (rows, cols, cols, rows)
    return jax.shard_map(body, mesh=physical, in_specs=in_specs, out_specs=out_specs, check_vma=False)
```
